512 devices in a mesh: req: 128 (over z, y, core), tp: 4 (over x).
Axes of the slice: x: 4, y: 4, z: 16, core: 2. Of those that a mesh axis runs over, the one named last changes fastest.
Arguments:
- states: bfloat16 [32768, 3072], P('req', 'tp'), may hold values from -12 to 12
- query_weight: bfloat16 [3072, 1536], P(None, 'tp'), may hold values from -0.75 to 0.75
- key_value_weight: bfloat16 [3072, 512], P(None, 'tp'), may hold values from -0.75 to 0.75
- lengths: int32 [128], P('req'), may hold values from 1 to 256, 16384 in all
- adapter_ids: int32 [128], P('req'), may hold values from 0 to 63, as said below
- adapter_slot: int32 [64], replicated, may hold values from 0 to 127, as said below
- down_store: bfloat16 [128, 3072, 32], P('req', 'tp'), may hold values from -0.109375 to 0.109375
- query_up_store: bfloat16 [128, 16, 1536], P('req', None, 'tp'), may hold values from -1.5 to 1.5
- key_value_store: bfloat16 [128, 16, 512], P('req', None, 'tp'), may hold values from -1.5 to 1.5
Outputs:
- context: bfloat16 [32768, 1536], P('req', 'tp')
The draws below stay inside these ranges and needn't reach their ends.
Inputs may be any that keep to these rules, and one draw needn't show every extreme that they name: `adapter_ids`: exactly 16 distinct adapters are named among all 128 requests. `adapter_slot`: distinct adapters have distinct rows.
All inputs are finite; a program needn't handle non-finite values. No bound on the sum of `lengths` on one device may be relied on, other than what follows from the above.
Results may differ from the reference program's by a relative error of at most 0.0072.
Values may be sent and summed in bfloat16 or wider, within the bound.
No kernel may reach another device: no remote copies, remote signals or barrier semaphores. Data moves between devices by JAX's collectives and lax.ppermute only.
A program may use at most 64 MiB of HBM per device.

```python
import math
import jax
import jax.numpy as jnp
import numpy as np
from jax import lax

D = 3072
HEADS = 12
KV_HEADS = 2
HEAD_DIM = 128
ADAPTER_RANK = 16
ADAPTERS = 64
ACTIVE = 16
SLOT = 256
REQS = 128
TOKENS = 32768
ADP_SLOTS = 128


def draw_states(key, part):
    first_key = jax.random.fold_in(key, 1)
    result = jnp.clip(jax.random.normal(first_key, (TOKENS, D), jnp.float32), -6.0, 6.0)
    return result.astype(jnp.bfloat16)


def draw_query_weight(key, part):
    independent = jax.random.normal(jax.random.fold_in(key, 12), (D, HEADS * HEAD_DIM), jnp.float32) / math.sqrt(D)
    result = independent
    return jnp.clip(result, -0.75, 0.75).astype(jnp.bfloat16)


def draw_key_value_weight(key, part):
    independent = jax.random.normal(jax.random.fold_in(key, 13), (D, 2 * KV_HEADS * HEAD_DIM), jnp.float32) / math.sqrt(D)
    result = independent
    return jnp.clip(result, -0.75, 0.75).astype(jnp.bfloat16)


def draw_adapter_ids(key, part):
    selected_adapters = jax.random.permutation(jax.random.fold_in(key, 21), ADAPTERS)[:ACTIVE]
    first_pick = jax.random.randint(jax.random.fold_in(key, 22), (REQS,), 0, ACTIVE)
    second_pick = jax.random.randint(jax.random.fold_in(key, 23), (REQS,), 0, ACTIVE)
    picks = jnp.minimum(first_pick, second_pick)
    ranks = jnp.arange(REQS)
    picks = jnp.where(ranks < ACTIVE, ranks, picks)
    picks = picks[jax.random.permutation(jax.random.fold_in(key, 24), REQS)]
    return selected_adapters[picks].astype(jnp.int32)


def draw_adapter_slot(key, part):
    return jax.random.permutation(jax.random.fold_in(key, 31), ADP_SLOTS)[:ADAPTERS].astype(jnp.int32)


def shard_levels(rng, shape, cuts, smallest, top_value):
    loudness = 1.0
    for dim, parts in cuts:
        steps = jax.random.uniform(jax.random.fold_in(jax.random.fold_in(rng, 6), dim), (parts,), jnp.float32, smallest / len(cuts), top_value / len(cuts))
        loudness = loudness * jnp.repeat(jnp.exp(steps), shape[dim] // parts).reshape((-1,) + (1,) * (len(shape) - 1 - dim))
    return loudness


def profile(count, total, limit, lean):
    weights = [(1 << 20) // math.isqrt(grade ** lean) + 1 for grade in range(2, count + 1)]
    rest, given = total - limit - (count - 1), [1] * (count - 1)
    while rest > 0:
        free = [i for i in range(count - 1) if given[i] < limit]
        mass, budget = sum([weights[i] for i in free]), rest
        for i in free:
            extra = min(limit - given[i], max(1, budget * weights[i] // mass), rest)
            given[i] = given[i] + extra
            rest = rest - extra
    return np.array([limit] + given)


def ragged(own_key, number_of, total, reach, lean):
    if number_of == 2:
        one = jax.random.randint(own_key, (), max(1, total - reach), min(reach, total - 1) + 1)
        return jnp.stack([one, total - one])
    tallies = jnp.asarray(profile(number_of, total, reach, lean), jnp.int32)
    twos = (number_of - 1) // 2
    source_of, taker = tallies[1:1 + 2 * twos:2], tallies[2:2 + 2 * twos:2]
    margin = jnp.minimum(source_of - 1, reach - taker)
    shifted = jax.random.randint(jax.random.fold_in(own_key, 1), (twos,), 0, 1 << 20) % (margin + 1)
    tallies = tallies.at[1:1 + 2 * twos:2].set(source_of - shifted).at[2:2 + 2 * twos:2].set(taker + shifted)
    return tallies[jax.random.permutation(jax.random.fold_in(own_key, 2), number_of)]


def noise(own_key, dims, width, most, shards=(), held_as=jnp.bfloat16):
    drawn = width * jax.random.normal(own_key, dims, jnp.float32)
    if shards:
        drawn = drawn * shard_levels(own_key, dims, shards, -0.22, 0.18)
    return jnp.clip(drawn, -most, most).astype(held_as)


def setup_inputs(seed: int = 0) -> dict:
    splits = jax.random.split(jax.random.key(seed), 10)
    return {
        "states": draw_states(jax.random.fold_in(splits[9], 71), 0),
        "query_weight": draw_query_weight(jax.random.fold_in(splits[9], 71), 0),
        "key_value_weight": draw_key_value_weight(jax.random.fold_in(splits[9], 71), 0),
        "lengths": ragged(splits[3], REQS, REQS * SLOT // 2, SLOT, 2).astype(jnp.int32),
        "adapter_ids": draw_adapter_ids(jax.random.fold_in(splits[9], 71), 0),
        "adapter_slot": draw_adapter_slot(jax.random.fold_in(splits[9], 71), 0),
        "down_store": noise(splits[6], (ADP_SLOTS, D, 2 * ADAPTER_RANK), D ** -0.5, 0.109375, ((0, 128), (1, 4))),
        "query_up_store": noise(splits[7], (ADP_SLOTS, ADAPTER_RANK, HEADS * HEAD_DIM), ADAPTER_RANK ** -0.5, 1.5, ((0, 128), (2, 4))),
        "key_value_store": noise(splits[8], (ADP_SLOTS, ADAPTER_RANK, 2 * KV_HEADS * HEAD_DIM), ADAPTER_RANK ** -0.5, 1.5, ((0, 128), (2, 4))),
    }


adapter_scale = 0.5
rope_base = 100000000000.0

def rotate(field):
    half = field.shape[-1] // 2
    count = field.shape[-3]
    position = jnp.arange(count).astype(jnp.float32)
    inverse = rope_base ** (-(jnp.arange(half).astype(jnp.float32) * 2.0) / field.shape[-1])
    angle = position[:, None] * inverse[None, :]
    cosine = jnp.cos(angle)[:, None, :]
    sine = jnp.sin(angle)[:, None, :]
    first_half = field[..., :half]
    second_half = field[..., half:]
    return jnp.concatenate([first_half * cosine - second_half * sine, second_half * cosine + first_half * sine], axis=-1)

def reference(states, query_weight, key_value_weight, lengths, adapter_ids, adapter_slot, down_store, query_up_store, key_value_store):
    group = HEADS // KV_HEADS
    key_width = KV_HEADS * HEAD_DIM
    scale = 1.0 / math.sqrt(HEAD_DIM)
    slots = adapter_slot[adapter_ids].astype(jnp.int32)
    blocks = states.reshape(REQS, SLOT, D)

    def one_request(item):
        token_states, selected_adapters, length = item
        rank_middle = jnp.dot(token_states, down_store[selected_adapters], preferred_element_type=jnp.float32).astype(jnp.bfloat16)
        query_plain = jnp.dot(token_states, query_weight, preferred_element_type=jnp.float32) + adapter_scale * jnp.dot(rank_middle[:, :ADAPTER_RANK], query_up_store[selected_adapters], preferred_element_type=jnp.float32)
        key_value_pair = (jnp.dot(token_states, key_value_weight, preferred_element_type=jnp.float32) + adapter_scale * jnp.dot(rank_middle[:, ADAPTER_RANK:], key_value_store[selected_adapters], preferred_element_type=jnp.float32)).astype(jnp.bfloat16)
        queries = rotate(query_plain.reshape(SLOT, HEADS, HEAD_DIM)).astype(jnp.bfloat16)
        keys = rotate(key_value_pair[:, :key_width].astype(jnp.float32).reshape(SLOT, KV_HEADS, HEAD_DIM)).astype(jnp.bfloat16)
        values = key_value_pair[:, key_width:].reshape(SLOT, KV_HEADS, HEAD_DIM)
        keys = jnp.repeat(keys, group, axis=1)
        values = jnp.repeat(values, group, axis=1)
        scores = jnp.einsum('qhd,khd->hqk', queries.astype(jnp.float32), keys.astype(jnp.float32)) * scale
        position = jnp.arange(SLOT, dtype=jnp.int32)
        allowed = (position[None, :] <= position[:, None]) & (position[None, :] < length)
        scores = jnp.where(allowed[None, :, :], scores, -jnp.inf)
        highest = lax.optimization_barrier(jnp.max(scores, axis=-1, keepdims=True))
        expo = jnp.exp(scores - highest)
        weights = (expo / lax.optimization_barrier(jnp.sum(expo, axis=-1, keepdims=True))).astype(jnp.bfloat16)
        context = jnp.einsum('hqk,khd->qhd', weights.astype(jnp.float32), values.astype(jnp.float32))
        context = jnp.where((position < length)[:, None, None], context, 0.0)
        return context.reshape(SLOT, HEADS * HEAD_DIM).astype(jnp.bfloat16)
    result = lax.map(one_request, (blocks, slots, lengths))
    return result.reshape(TOKENS, HEADS * HEAD_DIM)
```

```python
import math

import jax
import jax.numpy as jnp
from jax import lax
from jax.sharding import PartitionSpec as P

HEADS = 12
HEAD_DIM = 128
ACTIVE = 16


adapter_scale = 0.5
rope_base = 100000000000.0


def rotate(field):
    half = field.shape[-1] // 2
    count = field.shape[-3]
    position = jnp.arange(count).astype(jnp.float32)
    inverse = rope_base ** (-(jnp.arange(half).astype(jnp.float32) * 2.0) / field.shape[-1])
    angle = position[:, None] * inverse[None, :]
    cosine = jnp.cos(angle)[:, None, :]
    sine = jnp.sin(angle)[:, None, :]
    first_half = field[..., :half]
    second_half = field[..., half:]
    return jnp.concatenate(
        [first_half * cosine - second_half * sine, second_half * cosine + first_half * sine],
        axis=-1,
    )


def lookup_slots(wanted, adapter_slot):
    table = jnp.arange(adapter_slot.shape[0], dtype=jnp.int32)
    matches = wanted[:, None] == table[None, :]
    return jnp.sum(jnp.where(matches, adapter_slot[None, :], 0), axis=1)


def shifted(x, shift, n, pairs=None):
    if pairs is None:
        pairs = [(i, (i + shift) % n) for i in range(n)]
    return lax.ppermute(x, "tp", pairs)


def local(
    states,
    query_weight,
    key_value_weight,
    lengths,
    adapter_ids,
    adapter_slot,
    down_store,
    query_up_store,
    key_value_store,
):
    tp_index = lax.axis_index("tp")
    req_index = lax.axis_index("req")
    n_tp = lax.axis_size("tp")
    n_req = lax.axis_size("req")
    req_dev = lengths.shape[0]
    rows_total = states.shape[0]
    slot_len = rows_total // req_dev
    q_cols = query_weight.shape[1]
    kv_cols = key_value_weight.shape[1]
    heads_here = q_cols // HEAD_DIM
    store_rows = down_store.shape[0]

    ids_all = lax.all_gather(adapter_ids, "req", axis=0, tiled=True)
    slots_all = lookup_slots(ids_all, adapter_slot)
    slot_range = jnp.arange(store_rows * n_req, dtype=jnp.int32)
    used = jnp.any(slots_all[:, None] == slot_range[None, :], axis=0).astype(jnp.int32)
    prefix = jnp.sum(
        jnp.where(slot_range[None, :] < slot_range[:, None], used[None, :], 0), axis=1
    )
    own_rows = req_index * store_rows + jnp.arange(store_rows, dtype=jnp.int32)
    place = (jnp.arange(ACTIVE, dtype=jnp.int32)[None, :] == prefix[own_rows][:, None]) & (
        used[own_rows][:, None] > 0
    )

    def compact(member):
        picked = jnp.where(
            place[:, :, None, None], member[:, None, :, :], jnp.zeros((), member.dtype)
        )
        return jnp.sum(picked, axis=0)

    pooled = lax.psum(
        (compact(down_store), compact(query_up_store), compact(key_value_store)), "req"
    )
    own_slots = lookup_slots(adapter_ids, adapter_slot)
    own_k = prefix[own_slots]
    adapter_down, adapter_query, adapter_pair = (
        jnp.take(member, own_k, axis=0) for member in pooled
    )

    blocks = [states] + [shifted(states, s, n_tp) for s in range(1, n_tp)]
    stacked = jnp.stack(blocks, axis=0)
    source = (tp_index - jnp.arange(n_tp, dtype=jnp.int32)) % n_tp
    piece = jnp.take(stacked, source, axis=0)
    piece = jnp.transpose(piece, (1, 0, 2)).reshape(rows_total, -1)

    grouped_local = states.reshape(req_dev, slot_len, states.shape[1])
    rank_part = jnp.einsum(
        "rsd,rdk->rsk", grouped_local, adapter_down, preferred_element_type=jnp.float32
    )
    rank_sum = lax.optimization_barrier(lax.psum(rank_part, "tp"))
    rank_mid = rank_sum.astype(jnp.bfloat16)
    rank_cols = rank_mid.shape[2] // 2

    query_total = jnp.dot(piece, query_weight, preferred_element_type=jnp.float32)
    key_value_sum = jnp.dot(piece, key_value_weight, preferred_element_type=jnp.float32)
    query_addition = jnp.einsum(
        "rsk,rkc->rsc",
        rank_mid[:, :, :rank_cols],
        adapter_query,
        preferred_element_type=jnp.float32,
    ).reshape(rows_total, q_cols)
    key_value_extra = jnp.einsum(
        "rsk,rkc->rsc", rank_mid[:, :, rank_cols:], adapter_pair, preferred_element_type=jnp.float32
    ).reshape(rows_total, kv_cols)
    query_plain = query_total + adapter_scale * query_addition
    key_value_own = (key_value_sum + adapter_scale * key_value_extra).astype(jnp.bfloat16)

    from_left = shifted(key_value_own, 1, n_tp, [(0, 1), (1, 2)])
    from_right = shifted(key_value_own, -1, n_tp, [(2, 1), (3, 2)])
    from_far = shifted(key_value_own, 2, n_tp, [(1, 3), (2, 0)])
    key_block = jnp.where(
        tp_index == 0, key_value_own, jnp.where(tp_index == 3, from_far, from_left)
    )
    value_block = jnp.where(
        tp_index == 3, key_value_own, jnp.where(tp_index == 0, from_far, from_right)
    )

    queries = rotate(query_plain.reshape(req_dev, slot_len, heads_here, HEAD_DIM)).astype(
        jnp.bfloat16
    )
    keys_one = rotate(key_block.astype(jnp.float32).reshape(req_dev, slot_len, 1, HEAD_DIM)).astype(
        jnp.bfloat16
    )[:, :, 0, :]
    values_one = value_block.reshape(req_dev, slot_len, HEAD_DIM)
    scale = 1.0 / math.sqrt(HEAD_DIM)
    scores = (
        jnp.einsum("rqhd,rkd->rhqk", queries, keys_one, preferred_element_type=jnp.float32) * scale
    )
    position = jnp.arange(slot_len, dtype=jnp.int32)
    allowed = (position[None, None, :] <= position[None, :, None]) & (
        position[None, None, :] < lengths[:, None, None]
    )
    scores = jnp.where(allowed[:, None, :, :], scores, -jnp.inf)
    highest = jnp.max(scores, axis=-1, keepdims=True)
    expo = jnp.exp(scores - highest)
    weights = (expo / jnp.sum(expo, axis=-1, keepdims=True)).astype(jnp.bfloat16)
    context = jnp.einsum("rhqk,rkd->rqhd", weights, values_one, preferred_element_type=jnp.float32)
    live_rows = position[None, :] < lengths[:, None]
    context = jnp.where(live_rows[:, :, None, None], context, 0.0)
    return context.reshape(rows_total, q_cols).astype(jnp.bfloat16)


def solution(mesh):
    return jax.shard_map(
        local,
        mesh=mesh,
        in_specs=(
            P("req", "tp"),
            P(None, "tp"),
            P(None, "tp"),
            P("req"),
            P("req"),
            P(),
            P("req", "tp", None),
            P("req", None, "tp"),
            P("req", None, "tp"),
        ),
        out_specs=P("req", "tp"),
        check_vma=False,
    )
```

```python
import math

import jax
import jax.numpy as jnp
from jax import lax
from jax.sharding import PartitionSpec as P

HEADS = 12
HEAD_DIM = 128
ACTIVE = 16


adapter_scale = 0.5
rope_base = 100000000000.0


def rotate(field):
    half = field.shape[-1] // 2
    count = field.shape[-3]
    position = jnp.arange(count).astype(jnp.float32)
    inverse = rope_base ** (-(jnp.arange(half).astype(jnp.float32) * 2.0) / field.shape[-1])
    angle = position[:, None] * inverse[None, :]
    cosine = jnp.cos(angle)[:, None, :]
    sine = jnp.sin(angle)[:, None, :]
    first_half = field[..., :half]
    second_half = field[..., half:]
    return jnp.concatenate(
        [first_half * cosine - second_half * sine, second_half * cosine + first_half * sine],
        axis=-1,
    )


def lookup_slots(wanted, adapter_slot):
    table = jnp.arange(adapter_slot.shape[0], dtype=jnp.int32)
    matches = wanted[:, None] == table[None, :]
    return jnp.sum(jnp.where(matches, adapter_slot[None, :], 0), axis=1)


def shifted(x, shift, n, pairs=None, axis="tp"):
    if pairs is None:
        pairs = [(i, (i + shift) % n) for i in range(n)]
    return lax.ppermute(x, axis, pairs)


def doubled_sum(x, axis, n):
    step = 1
    while step < n:
        x = x + shifted(x, step, n, axis=axis)
        step *= 2
    return x


def local(
    states,
    query_weight,
    key_value_weight,
    lengths,
    adapter_ids,
    adapter_slot,
    down_store,
    query_up_store,
    key_value_store,
):
    tp_index = lax.axis_index("tp")
    iz = lax.axis_index("rz")
    iy = lax.axis_index("ry")
    n_tp = lax.axis_size("tp")
    nz = lax.axis_size("rz")
    ny = lax.axis_size("ry")
    n_req = nz * ny
    me = iz * ny + iy
    req_dev = lengths.shape[0]
    rows_total = states.shape[0]
    slot_len = rows_total // req_dev
    q_cols = query_weight.shape[1]
    kv_cols = key_value_weight.shape[1]
    heads_here = q_cols // HEAD_DIM
    store_rows = down_store.shape[0]
    assert req_dev == 1 and store_rows == 1 and ACTIVE % ny == 0

    own_slot = lookup_slots(adapter_ids, adapter_slot)
    req_range = jnp.arange(n_req, dtype=jnp.int32)
    slots_all = jnp.where(req_range == me, own_slot[0], 0)
    slots_all = doubled_sum(doubled_sum(slots_all, "ry", ny), "rz", nz)
    slot_range = jnp.arange(n_req * store_rows, dtype=jnp.int32)
    used = jnp.any(slots_all[:, None] == slot_range[None, :], axis=0).astype(jnp.int32)
    prefix = jnp.sum(
        jnp.where(slot_range[None, :] < slot_range[:, None], used[None, :], 0), axis=1
    )

    down_rows = down_store[0].T.reshape(-1, 128)
    query_rows = query_up_store[0].reshape(-1, 128)
    pair_rows = key_value_store[0].reshape(-1, 128)
    n_down, n_query = down_rows.shape[0], query_rows.shape[0]
    row = jnp.concatenate([down_rows, query_rows, pair_rows], axis=0)

    plane = jnp.stack([row] + [shifted(row, s, ny, axis="ry") for s in range(1, ny)])
    per_column = ACTIVE // ny
    back = jnp.arange(ny, dtype=jnp.int32)
    plane_slots = iz * ny + (iy - back) % ny
    wanted = iy + ny * jnp.arange(per_column, dtype=jnp.int32)
    choose = (used[plane_slots][None, :] > 0) & (prefix[plane_slots][None, :] == wanted[:, None])
    column = jnp.sum(
        jnp.where(choose[:, :, None, None], plane[None], jnp.zeros((), plane.dtype)), axis=1
    )
    column = doubled_sum(column, "rz", nz)
    gathered = jnp.stack([column] + [shifted(column, s, ny, axis="ry") for s in range(1, ny)])
    own_k = prefix[own_slot[0]]
    picked = gathered[(iy - own_k % ny) % ny, own_k // ny]
    down_t = picked[:n_down].reshape(down_store.shape[2], down_store.shape[1])
    adapter_query = picked[n_down:n_down + n_query].reshape(query_up_store.shape[1:])
    adapter_pair = picked[n_down + n_query:].reshape(key_value_store.shape[1:])

    blocks = [states] + [shifted(states, s, n_tp) for s in range(1, n_tp)]
    stacked = jnp.stack(blocks, axis=0)
    source = (tp_index - jnp.arange(n_tp, dtype=jnp.int32)) % n_tp
    piece = jnp.take(stacked, source, axis=0)
    piece = jnp.transpose(piece, (1, 0, 2)).reshape(rows_total, -1)

    rank_part = jnp.einsum("kd,sd->ks", down_t, states, preferred_element_type=jnp.float32)
    rank_sum = rank_part
    for s in range(1, n_tp):
        rank_sum = rank_sum + shifted(rank_part, s, n_tp)
    rank_mid = rank_sum.astype(jnp.bfloat16)
    rank_cols = rank_mid.shape[0] // 2

    query_total = jnp.dot(piece, query_weight, preferred_element_type=jnp.float32)
    key_value_sum = jnp.dot(piece, key_value_weight, preferred_element_type=jnp.float32)
    query_addition = jnp.einsum(
        "ks,kc->sc", rank_mid[:rank_cols], adapter_query, preferred_element_type=jnp.float32
    )
    key_value_extra = jnp.einsum(
        "ks,kc->sc", rank_mid[rank_cols:], adapter_pair, preferred_element_type=jnp.float32
    )
    query_plain = query_total + adapter_scale * query_addition
    key_value_own = (key_value_sum + adapter_scale * key_value_extra).astype(jnp.bfloat16)

    from_left = shifted(key_value_own, 1, n_tp, [(0, 1), (1, 2)])
    from_right = shifted(key_value_own, -1, n_tp, [(2, 1), (3, 2)])
    from_far = shifted(key_value_own, 2, n_tp, [(1, 3), (2, 0)])
    key_block = jnp.where(
        tp_index == 0, key_value_own, jnp.where(tp_index == 3, from_far, from_left)
    )
    value_block = jnp.where(
        tp_index == 3, key_value_own, jnp.where(tp_index == 0, from_far, from_right)
    )

    queries = rotate(query_plain.reshape(req_dev, slot_len, heads_here, HEAD_DIM)).astype(
        jnp.bfloat16
    )
    keys_one = rotate(key_block.astype(jnp.float32).reshape(req_dev, slot_len, 1, HEAD_DIM)).astype(
        jnp.bfloat16
    )[:, :, 0, :]
    values_one = value_block.reshape(req_dev, slot_len, HEAD_DIM)
    scale = 1.0 / math.sqrt(HEAD_DIM)
    scores = (
        jnp.einsum("rqhd,rkd->rhqk", queries, keys_one, preferred_element_type=jnp.float32) * scale
    )
    position = jnp.arange(slot_len, dtype=jnp.int32)
    allowed = (position[None, None, :] <= position[None, :, None]) & (
        position[None, None, :] < lengths[:, None, None]
    )
    scores = jnp.where(allowed[:, None, :, :], scores, -jnp.inf)
    highest = jnp.max(scores, axis=-1, keepdims=True)
    expo = jnp.exp(scores - highest)
    weights = (expo / jnp.sum(expo, axis=-1, keepdims=True)).astype(jnp.bfloat16)
    context = jnp.einsum("rhqk,rkd->rqhd", weights, values_one, preferred_element_type=jnp.float32)
    live_rows = position[None, :] < lengths[:, None]
    context = jnp.where(live_rows[:, :, None, None], context, 0.0)
    return context.reshape(rows_total, q_cols).astype(jnp.bfloat16)


def solution(mesh):
    n_req = mesh.shape["req"]
    ny = 8 if n_req % 8 == 0 else 1
    split = jax.sharding.Mesh(
        mesh.devices.reshape(n_req // ny, ny, mesh.shape["tp"]), ("rz", "ry", "tp")
    )
    req = ("rz", "ry")
    return jax.shard_map(
        local,
        mesh=split,
        in_specs=(
            P(req, "tp"),
            P(None, "tp"),
            P(None, "tp"),
            P(req),
            P(req),
            P(),
            P(req, "tp", None),
            P(req, None, "tp"),
            P(req, None, "tp"),
        ),
        out_specs=P(req, "tp"),
        check_vma=False,
    )
```

```python
import math

import jax
import jax.numpy as jnp
from jax import lax
from jax.sharding import PartitionSpec as P

HEADS = 12
HEAD_DIM = 128
ACTIVE = 16


adapter_scale = 0.5
rope_base = 100000000000.0


def rotate(field):
    half = field.shape[-1] // 2
    count = field.shape[-3]
    position = jnp.arange(count).astype(jnp.float32)
    inverse = rope_base ** (-(jnp.arange(half).astype(jnp.float32) * 2.0) / field.shape[-1])
    angle = position[:, None] * inverse[None, :]
    cosine = jnp.cos(angle)[:, None, :]
    sine = jnp.sin(angle)[:, None, :]
    first_half = field[..., :half]
    second_half = field[..., half:]
    return jnp.concatenate(
        [first_half * cosine - second_half * sine, second_half * cosine + first_half * sine],
        axis=-1,
    )


def lookup_slots(wanted, adapter_slot):
    table = jnp.arange(adapter_slot.shape[0], dtype=jnp.int32)
    matches = wanted[:, None] == table[None, :]
    return jnp.sum(jnp.where(matches, adapter_slot[None, :], 0), axis=1)


def shifted(x, shift, n, pairs=None, axis="tp"):
    if pairs is None:
        pairs = [(i, (i + shift) % n) for i in range(n)]
    return lax.ppermute(x, axis, pairs)


def spread_sum(x, axis, n, radix=4):
    step = 1
    while step < n:
        width = min(radix, n // step)
        assert n % (step * width) == 0
        terms = [x] + [shifted(x, step * m, n, axis=axis) for m in range(1, width)]
        x = sum(terms[1:], terms[0])
        step *= width
    return x


def local(
    states,
    query_weight,
    key_value_weight,
    lengths,
    adapter_ids,
    adapter_slot,
    down_store,
    query_up_store,
    key_value_store,
):
    tp_index = lax.axis_index("tp")
    iz = lax.axis_index("rz")
    iy = lax.axis_index("ry")
    n_tp = lax.axis_size("tp")
    nz = lax.axis_size("rz")
    ny = lax.axis_size("ry")
    n_req = nz * ny
    me = iz * ny + iy
    req_dev = lengths.shape[0]
    rows_total = states.shape[0]
    slot_len = rows_total // req_dev
    q_cols = query_weight.shape[1]
    kv_cols = key_value_weight.shape[1]
    heads_here = q_cols // HEAD_DIM
    store_rows = down_store.shape[0]
    assert req_dev == 1 and store_rows == 1 and ACTIVE % ny == 0

    own_slot = lookup_slots(adapter_ids, adapter_slot)

    down_rows = down_store[0].T.reshape(-1, 128)
    query_rows = query_up_store[0].reshape(-1, 128)
    pair_rows = key_value_store[0].reshape(-1, 128)
    n_down, n_query = down_rows.shape[0], query_rows.shape[0]
    n_row = n_down + n_query + pair_rows.shape[0]
    tag = jnp.zeros((8, 128), jnp.int32).at[0, 0].set(own_slot[0]).astype(down_rows.dtype)
    row = jnp.concatenate([down_rows, query_rows, pair_rows, tag], axis=0)

    plane = jnp.stack([row] + [shifted(row, s, ny, axis="ry") for s in range(1, ny)])
    back = jnp.arange(ny, dtype=jnp.int32)
    plane_req = iz * ny + (iy - back) % ny
    plane_tags = plane[:, n_row, 0].astype(jnp.int32)

    req_range = jnp.arange(n_req, dtype=jnp.int32)
    slots_all = jnp.sum(
        jnp.where(req_range[None, :] == plane_req[:, None], plane_tags[:, None], 0), axis=0
    )
    slots_all = spread_sum(slots_all, "rz", nz)
    slot_range = jnp.arange(n_req * store_rows, dtype=jnp.int32)
    used = jnp.any(slots_all[:, None] == slot_range[None, :], axis=0).astype(jnp.int32)
    prefix = jnp.sum(
        jnp.where(slot_range[None, :] < slot_range[:, None], used[None, :], 0), axis=1
    )

    per_column = ACTIVE // ny
    plane_slots = plane_req
    wanted = iy + ny * jnp.arange(per_column, dtype=jnp.int32)
    choose = (used[plane_slots][None, :] > 0) & (prefix[plane_slots][None, :] == wanted[:, None])
    column = jnp.sum(
        jnp.where(choose[:, :, None, None], plane[None, :, :n_row], jnp.zeros((), plane.dtype)),
        axis=1,
    )
    column = spread_sum(column, "rz", nz)
    gathered = jnp.stack([column] + [shifted(column, s, ny, axis="ry") for s in range(1, ny)])
    own_k = prefix[own_slot[0]]
    picked = gathered[(iy - own_k % ny) % ny, own_k // ny]
    down_t = picked[:n_down].reshape(down_store.shape[2], down_store.shape[1])
    adapter_query = picked[n_down:n_down + n_query].reshape(query_up_store.shape[1:])
    adapter_pair = picked[n_down + n_query:].reshape(key_value_store.shape[1:])

    blocks = [states] + [shifted(states, s, n_tp) for s in range(1, n_tp)]
    stacked = jnp.stack(blocks, axis=0)
    source = (tp_index - jnp.arange(n_tp, dtype=jnp.int32)) % n_tp
    piece = jnp.take(stacked, source, axis=0)
    piece = jnp.transpose(piece, (1, 0, 2)).reshape(rows_total, -1)

    rank_part = jnp.einsum("kd,sd->ks", down_t, states, preferred_element_type=jnp.float32)
    rank_sum = rank_part
    for s in range(1, n_tp):
        rank_sum = rank_sum + shifted(rank_part, s, n_tp)
    rank_mid = rank_sum.astype(jnp.bfloat16)
    rank_cols = rank_mid.shape[0] // 2

    query_total = jnp.dot(piece, query_weight, preferred_element_type=jnp.float32)
    key_value_sum = jnp.dot(piece, key_value_weight, preferred_element_type=jnp.float32)
    query_addition = jnp.einsum(
        "ks,kc->sc", rank_mid[:rank_cols], adapter_query, preferred_element_type=jnp.float32
    )
    key_value_extra = jnp.einsum(
        "ks,kc->sc", rank_mid[rank_cols:], adapter_pair, preferred_element_type=jnp.float32
    )
    query_plain = query_total + adapter_scale * query_addition
    key_value_own = (key_value_sum + adapter_scale * key_value_extra).astype(jnp.bfloat16)

    from_left = shifted(key_value_own, 1, n_tp, [(0, 1), (1, 2)])
    from_right = shifted(key_value_own, -1, n_tp, [(2, 1), (3, 2)])
    from_far = shifted(key_value_own, 2, n_tp, [(1, 3), (2, 0)])
    key_block = jnp.where(
        tp_index == 0, key_value_own, jnp.where(tp_index == 3, from_far, from_left)
    )
    value_block = jnp.where(
        tp_index == 3, key_value_own, jnp.where(tp_index == 0, from_far, from_right)
    )

    queries = rotate(query_plain.reshape(req_dev, slot_len, heads_here, HEAD_DIM)).astype(
        jnp.bfloat16
    )
    keys_one = rotate(key_block.astype(jnp.float32).reshape(req_dev, slot_len, 1, HEAD_DIM)).astype(
        jnp.bfloat16
    )[:, :, 0, :]
    values_one = value_block.reshape(req_dev, slot_len, HEAD_DIM)
    scale = 1.0 / math.sqrt(HEAD_DIM)
    scores = (
        jnp.einsum("rqhd,rkd->rhqk", queries, keys_one, preferred_element_type=jnp.float32) * scale
    )
    position = jnp.arange(slot_len, dtype=jnp.int32)
    allowed = (position[None, None, :] <= position[None, :, None]) & (
        position[None, None, :] < lengths[:, None, None]
    )
    scores = jnp.where(allowed[:, None, :, :], scores, -jnp.inf)
    highest = jnp.max(scores, axis=-1, keepdims=True)
    expo = jnp.exp(scores - highest)
    weights = (expo / jnp.sum(expo, axis=-1, keepdims=True)).astype(jnp.bfloat16)
    context = jnp.einsum("rhqk,rkd->rqhd", weights, values_one, preferred_element_type=jnp.float32)
    live_rows = position[None, :] < lengths[:, None]
    context = jnp.where(live_rows[:, :, None, None], context, 0.0)
    return context.reshape(rows_total, q_cols).astype(jnp.bfloat16)


def solution(mesh):
    n_req = mesh.shape["req"]
    ny = 8 if n_req % 8 == 0 else 1
    split = jax.sharding.Mesh(
        mesh.devices.reshape(n_req // ny, ny, mesh.shape["tp"]), ("rz", "ry", "tp")
    )
    req = ("rz", "ry")
    return jax.shard_map(
        local,
        mesh=split,
        in_specs=(
            P(req, "tp"),
            P(None, "tp"),
            P(None, "tp"),
            P(req),
            P(req),
            P(),
            P(req, "tp", None),
            P(req, None, "tp"),
            P(req, None, "tp"),
        ),
        out_specs=P(req, "tp"),
        check_vma=False,
    )
```

```python
import math

import jax
import jax.numpy as jnp
from jax import lax
from jax.sharding import PartitionSpec as P

HEADS = 12
HEAD_DIM = 128
ACTIVE = 16


adapter_scale = 0.5
rope_base = 100000000000.0


def rotate(field):
    half = field.shape[-1] // 2
    count = field.shape[-3]
    position = jnp.arange(count).astype(jnp.float32)
    inverse = rope_base ** (-(jnp.arange(half).astype(jnp.float32) * 2.0) / field.shape[-1])
    angle = position[:, None] * inverse[None, :]
    cosine = jnp.cos(angle)[:, None, :]
    sine = jnp.sin(angle)[:, None, :]
    first_half = field[..., :half]
    second_half = field[..., half:]
    return jnp.concatenate(
        [first_half * cosine - second_half * sine, second_half * cosine + first_half * sine],
        axis=-1,
    )


def lookup_slots(wanted, adapter_slot):
    table = jnp.arange(adapter_slot.shape[0], dtype=jnp.int32)
    matches = wanted[:, None] == table[None, :]
    return jnp.sum(jnp.where(matches, adapter_slot[None, :], 0), axis=1)


def shifted(x, shift, n, pairs=None, axis="tp"):
    if pairs is None:
        pairs = [(i, (i + shift) % n) for i in range(n)]
    return lax.ppermute(x, axis, pairs)


def gather_over(x, axis, n):
    copies = jnp.broadcast_to(x[None], (n,) + x.shape)
    return lax.all_to_all(copies, axis, 0, 0, tiled=True)


def spread_sum(x, axis, n, radix=4):
    step = 1
    while step < n:
        width = min(radix, n // step)
        assert n % (step * width) == 0
        terms = [x] + [shifted(x, step * m, n, axis=axis) for m in range(1, width)]
        x = sum(terms[1:], terms[0])
        step *= width
    return x


def local(
    states,
    query_weight,
    key_value_weight,
    lengths,
    adapter_ids,
    adapter_slot,
    down_store,
    query_up_store,
    key_value_store,
):
    tp_index = lax.axis_index("tp")
    iz = lax.axis_index("rz")
    iy = lax.axis_index("ry")
    n_tp = lax.axis_size("tp")
    nz = lax.axis_size("rz")
    ny = lax.axis_size("ry")
    n_req = nz * ny
    me = iz * ny + iy
    req_dev = lengths.shape[0]
    rows_total = states.shape[0]
    slot_len = rows_total // req_dev
    q_cols = query_weight.shape[1]
    kv_cols = key_value_weight.shape[1]
    heads_here = q_cols // HEAD_DIM
    store_rows = down_store.shape[0]
    assert req_dev == 1 and store_rows == 1 and ACTIVE % ny == 0

    own_slot = lookup_slots(adapter_ids, adapter_slot)

    down_rows = down_store[0].T.reshape(-1, 128)
    query_rows = query_up_store[0].reshape(-1, 128)
    pair_rows = key_value_store[0].reshape(-1, 128)
    n_down, n_query = down_rows.shape[0], query_rows.shape[0]
    n_row = n_down + n_query + pair_rows.shape[0]
    tag = jnp.zeros((8, 128), jnp.int32).at[0, 0].set(own_slot[0]).astype(down_rows.dtype)
    row = jnp.concatenate([down_rows, query_rows, pair_rows, tag], axis=0)

    plane = gather_over(row, "ry", ny)
    plane_req = iz * ny + jnp.arange(ny, dtype=jnp.int32)
    plane_tags = plane[:, n_row, 0].astype(jnp.int32)

    req_range = jnp.arange(n_req, dtype=jnp.int32)
    slots_all = jnp.sum(
        jnp.where(req_range[None, :] == plane_req[:, None], plane_tags[:, None], 0), axis=0
    )
    slots_all = spread_sum(slots_all, "rz", nz)
    slot_range = jnp.arange(n_req * store_rows, dtype=jnp.int32)
    used = jnp.any(slots_all[:, None] == slot_range[None, :], axis=0).astype(jnp.int32)
    prefix = jnp.sum(
        jnp.where(slot_range[None, :] < slot_range[:, None], used[None, :], 0), axis=1
    )

    per_column = ACTIVE // ny
    plane_slots = plane_req
    wanted = iy + ny * jnp.arange(per_column, dtype=jnp.int32)
    choose = (used[plane_slots][None, :] > 0) & (prefix[plane_slots][None, :] == wanted[:, None])
    column = jnp.sum(
        jnp.where(choose[:, :, None, None], plane[None, :, :n_row], jnp.zeros((), plane.dtype)),
        axis=1,
    )
    column = spread_sum(column, "rz", nz)
    gathered = gather_over(column, "ry", ny)
    own_k = prefix[own_slot[0]]
    picked = gathered[own_k % ny, own_k // ny]
    down_t = picked[:n_down].reshape(down_store.shape[2], down_store.shape[1])
    adapter_query = picked[n_down:n_down + n_query].reshape(query_up_store.shape[1:])
    adapter_pair = picked[n_down + n_query:].reshape(key_value_store.shape[1:])

    blocks = [states] + [shifted(states, s, n_tp) for s in range(1, n_tp)]
    stacked = jnp.stack(blocks, axis=0)
    source = (tp_index - jnp.arange(n_tp, dtype=jnp.int32)) % n_tp
    piece = jnp.take(stacked, source, axis=0)
    piece = jnp.transpose(piece, (1, 0, 2)).reshape(rows_total, -1)

    rank_part = jnp.einsum("kd,sd->ks", down_t, states, preferred_element_type=jnp.float32)
    rank_sum = rank_part
    for s in range(1, n_tp):
        rank_sum = rank_sum + shifted(rank_part, s, n_tp)
    rank_mid = rank_sum.astype(jnp.bfloat16)
    rank_cols = rank_mid.shape[0] // 2

    query_total = jnp.dot(piece, query_weight, preferred_element_type=jnp.float32)
    key_value_sum = jnp.dot(piece, key_value_weight, preferred_element_type=jnp.float32)
    query_addition = jnp.einsum(
        "ks,kc->sc", rank_mid[:rank_cols], adapter_query, preferred_element_type=jnp.float32
    )
    key_value_extra = jnp.einsum(
        "ks,kc->sc", rank_mid[rank_cols:], adapter_pair, preferred_element_type=jnp.float32
    )
    query_plain = query_total + adapter_scale * query_addition
    key_value_own = (key_value_sum + adapter_scale * key_value_extra).astype(jnp.bfloat16)

    from_left = shifted(key_value_own, 1, n_tp, [(0, 1), (1, 2)])
    from_right = shifted(key_value_own, -1, n_tp, [(2, 1), (3, 2)])
    from_far = shifted(key_value_own, 2, n_tp, [(1, 3), (2, 0)])
    key_block = jnp.where(
        tp_index == 0, key_value_own, jnp.where(tp_index == 3, from_far, from_left)
    )
    value_block = jnp.where(
        tp_index == 3, key_value_own, jnp.where(tp_index == 0, from_far, from_right)
    )

    queries = rotate(query_plain.reshape(req_dev, slot_len, heads_here, HEAD_DIM)).astype(
        jnp.bfloat16
    )
    keys_one = rotate(key_block.astype(jnp.float32).reshape(req_dev, slot_len, 1, HEAD_DIM)).astype(
        jnp.bfloat16
    )[:, :, 0, :]
    values_one = value_block.reshape(req_dev, slot_len, HEAD_DIM)
    scale = 1.0 / math.sqrt(HEAD_DIM)
    scores = (
        jnp.einsum("rqhd,rkd->rhqk", queries, keys_one, preferred_element_type=jnp.float32) * scale
    )
    position = jnp.arange(slot_len, dtype=jnp.int32)
    allowed = (position[None, None, :] <= position[None, :, None]) & (
        position[None, None, :] < lengths[:, None, None]
    )
    scores = jnp.where(allowed[:, None, :, :], scores, -jnp.inf)
    highest = jnp.max(scores, axis=-1, keepdims=True)
    expo = jnp.exp(scores - highest)
    weights = (expo / jnp.sum(expo, axis=-1, keepdims=True)).astype(jnp.bfloat16)
    context = jnp.einsum("rhqk,rkd->rqhd", weights, values_one, preferred_element_type=jnp.float32)
    live_rows = position[None, :] < lengths[:, None]
    context = jnp.where(live_rows[:, :, None, None], context, 0.0)
    return context.reshape(rows_total, q_cols).astype(jnp.bfloat16)


def solution(mesh):
    n_req = mesh.shape["req"]
    ny = 8 if n_req % 8 == 0 else 1
    split = jax.sharding.Mesh(
        mesh.devices.reshape(n_req // ny, ny, mesh.shape["tp"]), ("rz", "ry", "tp")
    )
    req = ("rz", "ry")
    return jax.shard_map(
        local,
        mesh=split,
        in_specs=(
            P(req, "tp"),
            P(None, "tp"),
            P(None, "tp"),
            P(req),
            P(req),
            P(),
            P(req, "tp", None),
            P(req, None, "tp"),
            P(req, None, "tp"),
        ),
        out_specs=P(req, "tp"),
        check_vma=False,
    )
```

```python
import math

import jax
import jax.numpy as jnp
from jax import lax
from jax.sharding import PartitionSpec as P

HEADS = 12
HEAD_DIM = 128
ACTIVE = 16


adapter_scale = 0.5
rope_base = 100000000000.0


def rotate(field):
    half = field.shape[-1] // 2
    count = field.shape[-3]
    position = jnp.arange(count).astype(jnp.float32)
    inverse = rope_base ** (-(jnp.arange(half).astype(jnp.float32) * 2.0) / field.shape[-1])
    angle = position[:, None] * inverse[None, :]
    cosine = jnp.cos(angle)[:, None, :]
    sine = jnp.sin(angle)[:, None, :]
    first_half = field[..., :half]
    second_half = field[..., half:]
    return jnp.concatenate(
        [first_half * cosine - second_half * sine, second_half * cosine + first_half * sine],
        axis=-1,
    )


def lookup_slots(wanted, adapter_slot):
    table = jnp.arange(adapter_slot.shape[0], dtype=jnp.int32)
    matches = wanted[:, None] == table[None, :]
    return jnp.sum(jnp.where(matches, adapter_slot[None, :], 0), axis=1)


def shifted(x, shift, n, pairs=None, axis="tp"):
    if pairs is None:
        pairs = [(i, (i + shift) % n) for i in range(n)]
    return lax.ppermute(x, axis, pairs)


def gather_over(x, axis, n):
    copies = jnp.broadcast_to(x[None], (n,) + x.shape)
    return lax.all_to_all(copies, axis, 0, 0, tiled=True)


def spread_sum(x, axis, n, radix=4):
    step = 1
    while step < n:
        width = min(radix, n // step)
        assert n % (step * width) == 0
        terms = [x] + [shifted(x, step * m, n, axis=axis) for m in range(1, width)]
        x = sum(terms[1:], terms[0])
        step *= width
    return x


def local(
    states,
    query_weight,
    key_value_weight,
    lengths,
    adapter_ids,
    adapter_slot,
    down_store,
    query_up_store,
    key_value_store,
):
    tp_index = lax.axis_index("tp")
    iz = lax.axis_index("rz")
    iy = lax.axis_index("ry")
    n_tp = lax.axis_size("tp")
    nz = lax.axis_size("rz")
    ny = lax.axis_size("ry")
    n_req = nz * ny
    me = iz * ny + iy
    req_dev = lengths.shape[0]
    rows_total = states.shape[0]
    slot_len = rows_total // req_dev
    q_cols = query_weight.shape[1]
    kv_cols = key_value_weight.shape[1]
    heads_here = q_cols // HEAD_DIM
    store_rows = down_store.shape[0]
    assert req_dev == 1 and store_rows == 1 and ACTIVE % ny == 0

    own_slot = lookup_slots(adapter_ids, adapter_slot)

    down_rows = down_store[0].T.reshape(-1, 128)
    query_rows = query_up_store[0].reshape(-1, 128)
    pair_rows = key_value_store[0].reshape(-1, 128)
    n_down, n_query = down_rows.shape[0], query_rows.shape[0]
    n_row = n_down + n_query + pair_rows.shape[0]
    tag = jnp.zeros((8, 128), jnp.int32).at[0, 0].set(own_slot[0]).astype(down_rows.dtype)
    row = jnp.concatenate([down_rows, query_rows, pair_rows, tag], axis=0)

    plane = gather_over(row, "ry", ny)
    plane_req = iz * ny + jnp.arange(ny, dtype=jnp.int32)
    plane_tags = plane[:, n_row, 0].astype(jnp.int32)

    slots_all = gather_over(plane_tags, "rz", nz).reshape(n_req)
    slot_range = jnp.arange(n_req * store_rows, dtype=jnp.int32)
    used = jnp.any(slots_all[:, None] == slot_range[None, :], axis=0).astype(jnp.int32)
    prefix = jnp.sum(
        jnp.where(slot_range[None, :] < slot_range[:, None], used[None, :], 0), axis=1
    )

    per_column = ACTIVE // ny
    plane_slots = plane_req
    wanted = iy + ny * jnp.arange(per_column, dtype=jnp.int32)
    choose = (used[plane_slots][None, :] > 0) & (prefix[plane_slots][None, :] == wanted[:, None])
    column = jnp.sum(
        jnp.where(choose[:, :, None, None], plane[None, :, :n_row], jnp.zeros((), plane.dtype)),
        axis=1,
    )
    column = spread_sum(column, "rz", nz)
    gathered = gather_over(column, "ry", ny)
    own_k = prefix[own_slot[0]]
    picked = gathered[own_k % ny, own_k // ny]
    down_t = picked[:n_down].reshape(down_store.shape[2], down_store.shape[1])
    adapter_query = picked[n_down:n_down + n_query].reshape(query_up_store.shape[1:])
    adapter_pair = picked[n_down + n_query:].reshape(key_value_store.shape[1:])

    blocks = [states] + [shifted(states, s, n_tp) for s in range(1, n_tp)]
    stacked = jnp.stack(blocks, axis=0)
    source = (tp_index - jnp.arange(n_tp, dtype=jnp.int32)) % n_tp
    piece = jnp.take(stacked, source, axis=0)
    piece = jnp.transpose(piece, (1, 0, 2)).reshape(rows_total, -1)

    rank_part = jnp.einsum("kd,sd->ks", down_t, states, preferred_element_type=jnp.float32)
    rank_sum = rank_part
    for s in range(1, n_tp):
        rank_sum = rank_sum + shifted(rank_part, s, n_tp)
    rank_mid = rank_sum.astype(jnp.bfloat16)
    rank_cols = rank_mid.shape[0] // 2

    query_total = jnp.dot(piece, query_weight, preferred_element_type=jnp.float32)
    key_value_sum = jnp.dot(piece, key_value_weight, preferred_element_type=jnp.float32)
    query_addition = jnp.einsum(
        "ks,kc->sc", rank_mid[:rank_cols], adapter_query, preferred_element_type=jnp.float32
    )
    key_value_extra = jnp.einsum(
        "ks,kc->sc", rank_mid[rank_cols:], adapter_pair, preferred_element_type=jnp.float32
    )
    query_plain = query_total + adapter_scale * query_addition
    key_value_own = (key_value_sum + adapter_scale * key_value_extra).astype(jnp.bfloat16)

    from_left = shifted(key_value_own, 1, n_tp, [(0, 1), (1, 2)])
    from_right = shifted(key_value_own, -1, n_tp, [(2, 1), (3, 2)])
    from_far = shifted(key_value_own, 2, n_tp, [(1, 3), (2, 0)])
    key_block = jnp.where(
        tp_index == 0, key_value_own, jnp.where(tp_index == 3, from_far, from_left)
    )
    value_block = jnp.where(
        tp_index == 3, key_value_own, jnp.where(tp_index == 0, from_far, from_right)
    )

    queries = rotate(query_plain.reshape(req_dev, slot_len, heads_here, HEAD_DIM)).astype(
        jnp.bfloat16
    )
    keys_one = rotate(key_block.astype(jnp.float32).reshape(req_dev, slot_len, 1, HEAD_DIM)).astype(
        jnp.bfloat16
    )[:, :, 0, :]
    values_one = value_block.reshape(req_dev, slot_len, HEAD_DIM)
    scale = 1.0 / math.sqrt(HEAD_DIM)
    scores = (
        jnp.einsum("rqhd,rkd->rhqk", queries, keys_one, preferred_element_type=jnp.float32) * scale
    )
    position = jnp.arange(slot_len, dtype=jnp.int32)
    allowed = (position[None, None, :] <= position[None, :, None]) & (
        position[None, None, :] < lengths[:, None, None]
    )
    scores = jnp.where(allowed[:, None, :, :], scores, -jnp.inf)
    highest = jnp.max(scores, axis=-1, keepdims=True)
    expo = jnp.exp(scores - highest)
    weights = (expo / jnp.sum(expo, axis=-1, keepdims=True)).astype(jnp.bfloat16)
    context = jnp.einsum("rhqk,rkd->rqhd", weights, values_one, preferred_element_type=jnp.float32)
    live_rows = position[None, :] < lengths[:, None]
    context = jnp.where(live_rows[:, :, None, None], context, 0.0)
    return context.reshape(rows_total, q_cols).astype(jnp.bfloat16)


def solution(mesh):
    n_req = mesh.shape["req"]
    ny = 8 if n_req % 8 == 0 else 1
    split = jax.sharding.Mesh(
        mesh.devices.reshape(n_req // ny, ny, mesh.shape["tp"]), ("rz", "ry", "tp")
    )
    req = ("rz", "ry")
    return jax.shard_map(
        local,
        mesh=split,
        in_specs=(
            P(req, "tp"),
            P(None, "tp"),
            P(None, "tp"),
            P(req),
            P(req),
            P(),
            P(req, "tp", None),
            P(req, None, "tp"),
            P(req, None, "tp"),
        ),
        out_specs=P(req, "tp"),
        check_vma=False,
    )
```

```python
import math

import jax
import jax.numpy as jnp
from jax import lax
from jax.sharding import PartitionSpec as P

HEADS = 12
HEAD_DIM = 128
ACTIVE = 16


adapter_scale = 0.5
rope_base = 100000000000.0


def rotate(field):
    half = field.shape[-1] // 2
    count = field.shape[-3]
    position = jnp.arange(count).astype(jnp.float32)
    inverse = rope_base ** (-(jnp.arange(half).astype(jnp.float32) * 2.0) / field.shape[-1])
    angle = position[:, None] * inverse[None, :]
    cosine = jnp.cos(angle)[:, None, :]
    sine = jnp.sin(angle)[:, None, :]
    first_half = field[..., :half]
    second_half = field[..., half:]
    return jnp.concatenate(
        [first_half * cosine - second_half * sine, second_half * cosine + first_half * sine],
        axis=-1,
    )


def lookup_slots(wanted, adapter_slot):
    table = jnp.arange(adapter_slot.shape[0], dtype=jnp.int32)
    matches = wanted[:, None] == table[None, :]
    return jnp.sum(jnp.where(matches, adapter_slot[None, :], 0), axis=1)


def shifted(x, shift, n, pairs=None, axis="tp"):
    if pairs is None:
        pairs = [(i, (i + shift) % n) for i in range(n)]
    return lax.ppermute(x, axis, pairs)


def gather_over(x, axis, n):
    copies = jnp.broadcast_to(x[None], (n,) + x.shape)
    return lax.all_to_all(copies, axis, 0, 0, tiled=True)


def spread_sum(x, axis, n, radix=4):
    step = 1
    while step < n:
        width = min(radix, n // step)
        assert n % (step * width) == 0
        terms = [x] + [shifted(x, step * m, n, axis=axis) for m in range(1, width)]
        x = sum(terms[1:], terms[0])
        step *= width
    return x


def local(
    states,
    query_weight,
    key_value_weight,
    lengths,
    adapter_ids,
    adapter_slot,
    down_store,
    query_up_store,
    key_value_store,
):
    tp_index = lax.axis_index("tp")
    iz = lax.axis_index("rz")
    iy = lax.axis_index("ry")
    n_tp = lax.axis_size("tp")
    nz = lax.axis_size("rz")
    ny = lax.axis_size("ry")
    n_req = nz * ny
    me = iz * ny + iy
    req_dev = lengths.shape[0]
    rows_total = states.shape[0]
    slot_len = rows_total // req_dev
    q_cols = query_weight.shape[1]
    kv_cols = key_value_weight.shape[1]
    heads_here = q_cols // HEAD_DIM
    store_rows = down_store.shape[0]
    assert req_dev == 1 and store_rows == 1 and ACTIVE % ny == 0

    own_slot = lookup_slots(adapter_ids, adapter_slot)

    down_rows = down_store[0].T.reshape(-1, 128)
    query_rows = query_up_store[0].reshape(-1, 128)
    pair_rows = key_value_store[0].reshape(-1, 128)
    n_down, n_query = down_rows.shape[0], query_rows.shape[0]
    n_row = n_down + n_query + pair_rows.shape[0]
    tag = jnp.zeros((8, 128), jnp.int32).at[0, 0].set(own_slot[0]).astype(down_rows.dtype)
    row = jnp.concatenate([down_rows, query_rows, pair_rows, tag], axis=0)

    plane = gather_over(row, "ry", ny)
    plane_req = iz * ny + jnp.arange(ny, dtype=jnp.int32)
    plane_tags = plane[:, n_row, 0].astype(jnp.int32)

    slots_all = gather_over(plane_tags, "rz", nz).reshape(n_req)
    slot_range = jnp.arange(n_req * store_rows, dtype=jnp.int32)
    used = jnp.any(slots_all[:, None] == slot_range[None, :], axis=0).astype(jnp.int32)
    prefix = jnp.sum(
        jnp.where(slot_range[None, :] < slot_range[:, None], used[None, :], 0), axis=1
    )

    per_column = ACTIVE // ny
    plane_slots = plane_req
    wanted = iy + ny * jnp.arange(per_column, dtype=jnp.int32)
    choose = (used[plane_slots][None, :] > 0) & (prefix[plane_slots][None, :] == wanted[:, None])
    column = jnp.sum(
        jnp.where(choose[:, :, None, None], plane[None, :, :n_row], jnp.zeros((), plane.dtype)),
        axis=1,
    )
    column = spread_sum(column, "rz", nz)
    gathered = gather_over(column, "ry", ny)
    own_k = prefix[own_slot[0]]
    picked = gathered[own_k % ny, own_k // ny]
    down_t = picked[:n_down].reshape(down_store.shape[2], down_store.shape[1])
    adapter_query = picked[n_down:n_down + n_query].reshape(query_up_store.shape[1:])
    adapter_pair = picked[n_down + n_query:].reshape(key_value_store.shape[1:])

    blocks = [states] + [shifted(states, s, n_tp) for s in range(1, n_tp)]
    stacked = jnp.stack(blocks, axis=0)
    source = (tp_index - jnp.arange(n_tp, dtype=jnp.int32)) % n_tp
    piece = jnp.take(stacked, source, axis=0)
    piece = jnp.transpose(piece, (1, 0, 2)).reshape(rows_total, -1)

    key_value_sum = jnp.dot(piece, key_value_weight, preferred_element_type=jnp.float32)
    from_left = shifted(key_value_sum, 1, n_tp, [(0, 1), (1, 2)])
    from_right = shifted(key_value_sum, -1, n_tp, [(2, 1), (3, 2)])
    from_far = shifted(key_value_sum, 2, n_tp, [(1, 3), (2, 0)])
    key_sum = jnp.where(
        tp_index == 0, key_value_sum, jnp.where(tp_index == 3, from_far, from_left)
    )
    value_sum = jnp.where(
        tp_index == 3, key_value_sum, jnp.where(tp_index == 0, from_far, from_right)
    )

    rank_part = jnp.einsum("kd,sd->ks", down_t, states, preferred_element_type=jnp.float32)
    n_rank = rank_part.shape[0]
    up_block = adapter_pair.astype(jnp.float32).reshape(-1, rank_part.shape[1])
    bundle = jnp.concatenate([rank_part, up_block], axis=0)
    arrived = [bundle] + [shifted(bundle, s, n_tp) for s in range(1, n_tp)]
    rank_sum = arrived[0][:n_rank]
    for part in arrived[1:]:
        rank_sum = rank_sum + part[:n_rank]
    rank_mid = rank_sum.astype(jnp.bfloat16)
    rank_cols = rank_mid.shape[0] // 2
    up_all = jnp.stack([part[n_rank:] for part in arrived]).astype(jnp.bfloat16)
    up_all = up_all.reshape((n_tp,) + adapter_pair.shape)
    kv_heads = (n_tp * kv_cols) // 2 // HEAD_DIM
    group_index = tp_index * heads_here // (HEADS // kv_heads)
    key_up = up_all[(tp_index - group_index) % n_tp]
    value_up = up_all[(tp_index - kv_heads - group_index) % n_tp]

    query_total = jnp.dot(piece, query_weight, preferred_element_type=jnp.float32)
    query_addition = jnp.einsum(
        "ks,kc->sc", rank_mid[:rank_cols], adapter_query, preferred_element_type=jnp.float32
    )
    query_plain = query_total + adapter_scale * query_addition
    key_extra = jnp.einsum(
        "ks,kc->sc", rank_mid[rank_cols:], key_up, preferred_element_type=jnp.float32
    )
    value_extra = jnp.einsum(
        "ks,kc->sc", rank_mid[rank_cols:], value_up, preferred_element_type=jnp.float32
    )
    key_block = (key_sum + adapter_scale * key_extra).astype(jnp.bfloat16)
    value_block = (value_sum + adapter_scale * value_extra).astype(jnp.bfloat16)

    queries = rotate(query_plain.reshape(req_dev, slot_len, heads_here, HEAD_DIM)).astype(
        jnp.bfloat16
    )
    keys_one = rotate(key_block.astype(jnp.float32).reshape(req_dev, slot_len, 1, HEAD_DIM)).astype(
        jnp.bfloat16
    )[:, :, 0, :]
    values_one = value_block.reshape(req_dev, slot_len, HEAD_DIM)
    scale = 1.0 / math.sqrt(HEAD_DIM)
    scores = (
        jnp.einsum("rqhd,rkd->rhqk", queries, keys_one, preferred_element_type=jnp.float32) * scale
    )
    position = jnp.arange(slot_len, dtype=jnp.int32)
    allowed = (position[None, None, :] <= position[None, :, None]) & (
        position[None, None, :] < lengths[:, None, None]
    )
    scores = jnp.where(allowed[:, None, :, :], scores, -jnp.inf)
    highest = jnp.max(scores, axis=-1, keepdims=True)
    expo = jnp.exp(scores - highest)
    weights = (expo / jnp.sum(expo, axis=-1, keepdims=True)).astype(jnp.bfloat16)
    context = jnp.einsum("rhqk,rkd->rqhd", weights, values_one, preferred_element_type=jnp.float32)
    live_rows = position[None, :] < lengths[:, None]
    context = jnp.where(live_rows[:, :, None, None], context, 0.0)
    return context.reshape(rows_total, q_cols).astype(jnp.bfloat16)


def solution(mesh):
    n_req = mesh.shape["req"]
    ny = 8 if n_req % 8 == 0 else 1
    split = jax.sharding.Mesh(
        mesh.devices.reshape(n_req // ny, ny, mesh.shape["tp"]), ("rz", "ry", "tp")
    )
    req = ("rz", "ry")
    return jax.shard_map(
        local,
        mesh=split,
        in_specs=(
            P(req, "tp"),
            P(None, "tp"),
            P(None, "tp"),
            P(req),
            P(req),
            P(),
            P(req, "tp", None),
            P(req, None, "tp"),
            P(req, None, "tp"),
        ),
        out_specs=P(req, "tp"),
        check_vma=False,
    )
```

```python
import math

import jax
import jax.numpy as jnp
from jax import lax
from jax.sharding import PartitionSpec as P

HEADS = 12
HEAD_DIM = 128
ACTIVE = 16


adapter_scale = 0.5
rope_base = 100000000000.0


def rotate(field):
    half = field.shape[-1] // 2
    count = field.shape[-3]
    position = jnp.arange(count).astype(jnp.float32)
    inverse = rope_base ** (-(jnp.arange(half).astype(jnp.float32) * 2.0) / field.shape[-1])
    angle = position[:, None] * inverse[None, :]
    cosine = jnp.cos(angle)[:, None, :]
    sine = jnp.sin(angle)[:, None, :]
    first_half = field[..., :half]
    second_half = field[..., half:]
    return jnp.concatenate(
        [first_half * cosine - second_half * sine, second_half * cosine + first_half * sine],
        axis=-1,
    )


def lookup_slots(wanted, adapter_slot):
    table = jnp.arange(adapter_slot.shape[0], dtype=jnp.int32)
    matches = wanted[:, None] == table[None, :]
    return jnp.sum(jnp.where(matches, adapter_slot[None, :], 0), axis=1)


def shifted(x, shift, n, pairs=None, axis="tp"):
    if pairs is None:
        pairs = [(i, (i + shift) % n) for i in range(n)]
    return lax.ppermute(x, axis, pairs)


def gather_over(x, axis, n):
    copies = jnp.broadcast_to(x[None], (n,) + x.shape)
    return lax.all_to_all(copies, axis, 0, 0, tiled=True)


def spread_sum(x, axis, n, radix=4):
    step = 1
    while step < n:
        width = min(radix, n // step)
        assert n % (step * width) == 0
        terms = [x] + [shifted(x, step * m, n, axis=axis) for m in range(1, width)]
        x = sum(terms[1:], terms[0])
        step *= width
    return x


def local(
    states,
    query_weight,
    key_value_weight,
    lengths,
    adapter_ids,
    adapter_slot,
    down_store,
    query_up_store,
    key_value_store,
):
    tp_index = lax.axis_index("tp")
    iz = lax.axis_index("rz")
    iy = lax.axis_index("ry")
    n_tp = lax.axis_size("tp")
    nz = lax.axis_size("rz")
    ny = lax.axis_size("ry")
    n_req = nz * ny
    me = iz * ny + iy
    req_dev = lengths.shape[0]
    rows_total = states.shape[0]
    slot_len = rows_total // req_dev
    q_cols = query_weight.shape[1]
    kv_cols = key_value_weight.shape[1]
    heads_here = q_cols // HEAD_DIM
    store_rows = down_store.shape[0]
    assert req_dev == 1 and store_rows == 1 and ACTIVE % ny == 0

    own_slot = lookup_slots(adapter_ids, adapter_slot)

    slots_all = gather_over(own_slot, ("rz", "ry"), n_req).reshape(n_req)

    down_rows = down_store[0].T.reshape(-1, 128)
    query_rows = query_up_store[0].reshape(-1, 128)
    pair_rows = key_value_store[0].reshape(-1, 128)
    n_down, n_query = down_rows.shape[0], query_rows.shape[0]
    n_row = n_down + n_query + pair_rows.shape[0]
    row = jnp.concatenate([down_rows, query_rows, pair_rows], axis=0)

    plane = gather_over(row, "ry", ny)
    plane_req = iz * ny + jnp.arange(ny, dtype=jnp.int32)

    slot_range = jnp.arange(n_req * store_rows, dtype=jnp.int32)
    used = jnp.any(slots_all[:, None] == slot_range[None, :], axis=0).astype(jnp.int32)
    prefix = jnp.sum(
        jnp.where(slot_range[None, :] < slot_range[:, None], used[None, :], 0), axis=1
    )

    per_column = ACTIVE // ny
    plane_slots = plane_req
    wanted = iy + ny * jnp.arange(per_column, dtype=jnp.int32)
    choose = (used[plane_slots][None, :] > 0) & (prefix[plane_slots][None, :] == wanted[:, None])
    column = jnp.sum(
        jnp.where(choose[:, :, None, None], plane[None], jnp.zeros((), plane.dtype)),
        axis=1,
    )
    column = spread_sum(column, "rz", nz)
    gathered = gather_over(column, "ry", ny)
    own_k = prefix[own_slot[0]]
    picked = gathered[own_k % ny, own_k // ny]
    down_t = picked[:n_down].reshape(down_store.shape[2], down_store.shape[1])
    adapter_query = picked[n_down:n_down + n_query].reshape(query_up_store.shape[1:])
    adapter_pair = picked[n_down + n_query:].reshape(key_value_store.shape[1:])

    piece = gather_over(states, "tp", n_tp)
    piece = jnp.transpose(piece, (1, 0, 2)).reshape(rows_total, -1)

    key_value_sum = jnp.dot(piece, key_value_weight, preferred_element_type=jnp.float32)

    rank_part = jnp.einsum("kd,sd->ks", down_t, states, preferred_element_type=jnp.float32)
    n_rank, width = rank_part.shape
    up_block = adapter_pair.astype(jnp.float32).reshape(-1, width)
    n_up = up_block.shape[0]
    bundle = jnp.concatenate([rank_part, up_block, key_value_sum.reshape(-1, width)], axis=0)
    arrived = gather_over(bundle, "tp", n_tp)
    rank_sum = arrived[0, :n_rank]
    for d in range(1, n_tp):
        rank_sum = rank_sum + arrived[d, :n_rank]
    rank_mid = rank_sum.astype(jnp.bfloat16)
    rank_cols = rank_mid.shape[0] // 2
    up_all = arrived[:, n_rank:n_rank + n_up].astype(jnp.bfloat16)
    up_all = up_all.reshape((n_tp,) + adapter_pair.shape)
    base_all = arrived[:, n_rank + n_up:].reshape((n_tp,) + key_value_sum.shape)
    kv_heads = (n_tp * kv_cols) // 2 // HEAD_DIM
    group_index = tp_index * heads_here // (HEADS // kv_heads)
    key_up = up_all[group_index]
    value_up = up_all[kv_heads + group_index]
    key_sum = base_all[group_index]
    value_sum = base_all[kv_heads + group_index]

    query_total = jnp.dot(piece, query_weight, preferred_element_type=jnp.float32)
    query_addition = jnp.einsum(
        "ks,kc->sc", rank_mid[:rank_cols], adapter_query, preferred_element_type=jnp.float32
    )
    query_plain = query_total + adapter_scale * query_addition
    key_extra = jnp.einsum(
        "ks,kc->sc", rank_mid[rank_cols:], key_up, preferred_element_type=jnp.float32
    )
    value_extra = jnp.einsum(
        "ks,kc->sc", rank_mid[rank_cols:], value_up, preferred_element_type=jnp.float32
    )
    key_block = lax.reduce_precision(
        key_sum + adapter_scale * key_extra, exponent_bits=8, mantissa_bits=7
    )
    value_block = (value_sum + adapter_scale * value_extra).astype(jnp.bfloat16)

    queries = rotate(query_plain.reshape(req_dev, slot_len, heads_here, HEAD_DIM)).astype(
        jnp.bfloat16
    )
    keys_one = rotate(key_block.reshape(req_dev, slot_len, 1, HEAD_DIM)).astype(
        jnp.bfloat16
    )[:, :, 0, :]
    values_one = value_block.reshape(req_dev, slot_len, HEAD_DIM)
    scale = 1.0 / math.sqrt(HEAD_DIM)
    scores = (
        jnp.einsum("rqhd,rkd->rhqk", queries, keys_one, preferred_element_type=jnp.float32) * scale
    )
    position = jnp.arange(slot_len, dtype=jnp.int32)
    allowed = (position[None, None, :] <= position[None, :, None]) & (
        position[None, None, :] < lengths[:, None, None]
    )
    scores = jnp.where(allowed[:, None, :, :], scores, -jnp.inf)
    highest = jnp.max(scores, axis=-1, keepdims=True)
    expo = jnp.exp(scores - highest)
    weights = (expo / jnp.sum(expo, axis=-1, keepdims=True)).astype(jnp.bfloat16)
    context = jnp.einsum("rhqk,rkd->rqhd", weights, values_one, preferred_element_type=jnp.float32)
    live_rows = position[None, :] < lengths[:, None]
    context = jnp.where(live_rows[:, :, None, None], context, 0.0)
    return context.reshape(rows_total, q_cols).astype(jnp.bfloat16)


def solution(mesh):
    n_req = mesh.shape["req"]
    ny = 8 if n_req % 8 == 0 else 1
    split = jax.sharding.Mesh(
        mesh.devices.reshape(n_req // ny, ny, mesh.shape["tp"]), ("rz", "ry", "tp")
    )
    req = ("rz", "ry")
    return jax.shard_map(
        local,
        mesh=split,
        in_specs=(
            P(req, "tp"),
            P(None, "tp"),
            P(None, "tp"),
            P(req),
            P(req),
            P(),
            P(req, "tp", None),
            P(req, None, "tp"),
            P(req, None, "tp"),
        ),
        out_specs=P(req, "tp"),
        check_vma=False,
    )
```

```python
import math

import jax
import jax.numpy as jnp
from jax import lax
from jax.sharding import PartitionSpec as P

HEADS = 12
HEAD_DIM = 128
ACTIVE = 16


adapter_scale = 0.5
rope_base = 100000000000.0


def rotate(field):
    half = field.shape[-1] // 2
    count = field.shape[-3]
    position = jnp.arange(count).astype(jnp.float32)
    inverse = rope_base ** (-(jnp.arange(half).astype(jnp.float32) * 2.0) / field.shape[-1])
    angle = position[:, None] * inverse[None, :]
    cosine = jnp.cos(angle)[:, None, :]
    sine = jnp.sin(angle)[:, None, :]
    first_half = field[..., :half]
    second_half = field[..., half:]
    return jnp.concatenate(
        [first_half * cosine - second_half * sine, second_half * cosine + first_half * sine],
        axis=-1,
    )


def lookup_slots(wanted, adapter_slot):
    table = jnp.arange(adapter_slot.shape[0], dtype=jnp.int32)
    matches = wanted[:, None] == table[None, :]
    return jnp.sum(jnp.where(matches, adapter_slot[None, :], 0), axis=1)


def shifted(x, shift, n, pairs=None, axis="tp"):
    if pairs is None:
        pairs = [(i, (i + shift) % n) for i in range(n)]
    return lax.ppermute(x, axis, pairs)


def gather_over(x, axis, n):
    copies = jnp.broadcast_to(x[None], (n,) + x.shape)
    return lax.all_to_all(copies, axis, 0, 0, tiled=True)


def spread_sum(x, axis, n, radix=4):
    step = 1
    while step < n:
        width = min(radix, n // step)
        assert n % (step * width) == 0
        terms = [x] + [shifted(x, step * m, n, axis=axis) for m in range(1, width)]
        x = sum(terms[1:], terms[0])
        step *= width
    return x


def local(
    states,
    query_weight,
    key_value_weight,
    lengths,
    adapter_ids,
    adapter_slot,
    down_store,
    query_up_store,
    key_value_store,
):
    tp_index = lax.axis_index("tp")
    iz = lax.axis_index("rz")
    iy = lax.axis_index("ry")
    n_tp = lax.axis_size("tp")
    nz = lax.axis_size("rz")
    ny = lax.axis_size("ry")
    n_req = nz * ny
    me = iz * ny + iy
    req_dev = lengths.shape[0]
    rows_total = states.shape[0]
    slot_len = rows_total // req_dev
    q_cols = query_weight.shape[1]
    kv_cols = key_value_weight.shape[1]
    heads_here = q_cols // HEAD_DIM
    store_rows = down_store.shape[0]
    assert req_dev == 1 and store_rows == 1 and ACTIVE % ny == 0

    own_slot = lookup_slots(adapter_ids, adapter_slot)

    slots_all = gather_over(own_slot, ("rz", "ry"), n_req).reshape(n_req)

    down_rows = down_store[0].T.reshape(-1, 128)
    query_rows = query_up_store[0].reshape(-1, 128)
    pair_rows = key_value_store[0].reshape(-1, 128)
    n_down, n_query = down_rows.shape[0], query_rows.shape[0]
    n_row = n_down + n_query + pair_rows.shape[0]
    row = jnp.concatenate([down_rows, query_rows, pair_rows], axis=0)

    plane = gather_over(row, "ry", ny)
    plane_req = iz * ny + jnp.arange(ny, dtype=jnp.int32)

    slot_range = jnp.arange(n_req * store_rows, dtype=jnp.int32)
    used = jnp.any(slots_all[:, None] == slot_range[None, :], axis=0).astype(jnp.int32)
    prefix = jnp.sum(
        jnp.where(slot_range[None, :] < slot_range[:, None], used[None, :], 0), axis=1
    )

    per_column = ACTIVE // ny
    plane_slots = plane_req
    wanted = iy + ny * jnp.arange(per_column, dtype=jnp.int32)
    choose = (used[plane_slots][None, :] > 0) & (prefix[plane_slots][None, :] == wanted[:, None])
    column = jnp.sum(
        jnp.where(choose[:, :, None, None], plane[None], jnp.zeros((), plane.dtype)),
        axis=1,
    )
    column = spread_sum(column, "rz", nz)
    dest_k = prefix[slots_all[plane_req]]
    held = column[0]
    for m in range(1, per_column):
        held = jnp.where((dest_k // ny == m)[:, None, None], column[m], held)
    send = jnp.where((dest_k % ny == iy)[:, None, None], held, jnp.zeros((), held.dtype))
    received = lax.all_to_all(send, "ry", 0, 0, tiled=True)
    own_k = prefix[own_slot[0]]
    picked = received[own_k % ny]
    down_t = picked[:n_down].reshape(down_store.shape[2], down_store.shape[1])
    adapter_query = picked[n_down:n_down + n_query].reshape(query_up_store.shape[1:])
    adapter_pair = picked[n_down + n_query:].reshape(key_value_store.shape[1:])

    piece = gather_over(states, "tp", n_tp)
    piece = jnp.transpose(piece, (1, 0, 2)).reshape(rows_total, -1)

    key_value_sum = jnp.dot(piece, key_value_weight, preferred_element_type=jnp.float32)

    rank_part = jnp.einsum("kd,sd->ks", down_t, states, preferred_element_type=jnp.float32)
    n_rank, width = rank_part.shape
    lanes = key_value_sum.shape[1]
    rank_rows = rank_part.reshape(-1, lanes)
    n_mid, n_up = rank_rows.shape[0], adapter_pair.shape[0]
    bundle = jnp.concatenate(
        [rank_rows, adapter_pair.astype(jnp.float32), key_value_sum], axis=0
    )
    arrived = gather_over(bundle, "tp", n_tp)
    rank_sum = arrived[0, :n_mid]
    for d in range(1, n_tp):
        rank_sum = rank_sum + arrived[d, :n_mid]
    rank_mid = rank_sum.reshape(n_rank, width).astype(jnp.bfloat16)
    rank_cols = rank_mid.shape[0] // 2
    up_all = arrived[:, n_mid:n_mid + n_up].astype(jnp.bfloat16)
    base_all = arrived[:, n_mid + n_up:]
    kv_heads = (n_tp * kv_cols) // 2 // HEAD_DIM
    group_index = tp_index * heads_here // (HEADS // kv_heads)
    key_up = up_all[group_index]
    value_up = up_all[kv_heads + group_index]
    key_sum = base_all[group_index]
    value_sum = base_all[kv_heads + group_index]

    query_total = jnp.dot(piece, query_weight, preferred_element_type=jnp.float32)
    query_addition = jnp.einsum(
        "ks,kc->sc", rank_mid[:rank_cols], adapter_query, preferred_element_type=jnp.float32
    )
    query_plain = query_total + adapter_scale * query_addition
    key_extra = jnp.einsum(
        "ks,kc->sc", rank_mid[rank_cols:], key_up, preferred_element_type=jnp.float32
    )
    value_extra = jnp.einsum(
        "ks,kc->sc", rank_mid[rank_cols:], value_up, preferred_element_type=jnp.float32
    )
    key_block = lax.reduce_precision(
        key_sum + adapter_scale * key_extra, exponent_bits=8, mantissa_bits=7
    )
    value_block = (value_sum + adapter_scale * value_extra).astype(jnp.bfloat16)

    queries = rotate(query_plain.reshape(req_dev, slot_len, heads_here, HEAD_DIM)).astype(
        jnp.bfloat16
    )
    keys_one = rotate(key_block.reshape(req_dev, slot_len, 1, HEAD_DIM)).astype(
        jnp.bfloat16
    )[:, :, 0, :]
    values_one = value_block.reshape(req_dev, slot_len, HEAD_DIM)
    scale = 1.0 / math.sqrt(HEAD_DIM)
    scores = (
        jnp.einsum("rqhd,rkd->rhqk", queries, keys_one, preferred_element_type=jnp.float32) * scale
    )
    position = jnp.arange(slot_len, dtype=jnp.int32)
    allowed = (position[None, None, :] <= position[None, :, None]) & (
        position[None, None, :] < lengths[:, None, None]
    )
    scores = jnp.where(allowed[:, None, :, :], scores, -jnp.inf)
    highest = jnp.max(scores, axis=-1, keepdims=True)
    expo = jnp.exp(scores - highest)
    weights = (expo / jnp.sum(expo, axis=-1, keepdims=True)).astype(jnp.bfloat16)
    context = jnp.einsum("rhqk,rkd->rqhd", weights, values_one, preferred_element_type=jnp.float32)
    live_rows = position[None, :] < lengths[:, None]
    context = jnp.where(live_rows[:, :, None, None], context, 0.0)
    return context.reshape(rows_total, q_cols).astype(jnp.bfloat16)


def solution(mesh):
    n_req = mesh.shape["req"]
    ny = 8 if n_req % 8 == 0 else 1
    split = jax.sharding.Mesh(
        mesh.devices.reshape(n_req // ny, ny, mesh.shape["tp"]), ("rz", "ry", "tp")
    )
    req = ("rz", "ry")
    return jax.shard_map(
        local,
        mesh=split,
        in_specs=(
            P(req, "tp"),
            P(None, "tp"),
            P(None, "tp"),
            P(req),
            P(req),
            P(),
            P(req, "tp", None),
            P(req, None, "tp"),
            P(req, None, "tp"),
        ),
        out_specs=P(req, "tp"),
        check_vma=False,
    )
```

```python
import math

import jax
import jax.numpy as jnp
from jax import lax
from jax.sharding import PartitionSpec as P

HEADS = 12
HEAD_DIM = 128
ACTIVE = 16


adapter_scale = 0.5
rope_base = 100000000000.0


def rotate(field):
    half = field.shape[-1] // 2
    count = field.shape[-3]
    position = jnp.arange(count).astype(jnp.float32)
    inverse = rope_base ** (-(jnp.arange(half).astype(jnp.float32) * 2.0) / field.shape[-1])
    angle = position[:, None] * inverse[None, :]
    cosine = jnp.cos(angle)[:, None, :]
    sine = jnp.sin(angle)[:, None, :]
    first_half = field[..., :half]
    second_half = field[..., half:]
    return jnp.concatenate(
        [first_half * cosine - second_half * sine, second_half * cosine + first_half * sine],
        axis=-1,
    )


def lookup_slots(wanted, adapter_slot):
    table = jnp.arange(adapter_slot.shape[0], dtype=jnp.int32)
    matches = wanted[:, None] == table[None, :]
    return jnp.sum(jnp.where(matches, adapter_slot[None, :], 0), axis=1)


def shifted(x, shift, n, pairs=None, axis="tp"):
    if pairs is None:
        pairs = [(i, (i + shift) % n) for i in range(n)]
    return lax.ppermute(x, axis, pairs)


def gather_over(x, axis, n):
    copies = jnp.broadcast_to(x[None], (n,) + x.shape)
    return lax.all_to_all(copies, axis, 0, 0, tiled=True)


def spread_sum(x, axis, n, radix=4):
    step = 1
    while step < n:
        width = min(radix, n // step)
        assert n % (step * width) == 0
        terms = [x] + [shifted(x, step * m, n, axis=axis) for m in range(1, width)]
        x = sum(terms[1:], terms[0])
        step *= width
    return x


def local(
    states,
    query_weight,
    key_value_weight,
    lengths,
    adapter_ids,
    adapter_slot,
    down_store,
    query_up_store,
    key_value_store,
):
    tp_index = lax.axis_index("tp")
    iz = lax.axis_index("rz")
    iy = lax.axis_index("ry")
    n_tp = lax.axis_size("tp")
    nz = lax.axis_size("rz")
    ny = lax.axis_size("ry")
    n_req = nz * ny
    me = iz * ny + iy
    req_dev = lengths.shape[0]
    rows_total = states.shape[0]
    slot_len = rows_total // req_dev
    q_cols = query_weight.shape[1]
    kv_cols = key_value_weight.shape[1]
    heads_here = q_cols // HEAD_DIM
    store_rows = down_store.shape[0]
    assert req_dev == 1 and store_rows == 1 and ACTIVE % ny == 0

    own_slot = lookup_slots(adapter_ids, adapter_slot)

    slots_all = gather_over(own_slot, ("rz", "ry"), n_req).reshape(n_req)

    down_rows = down_store[0].T.reshape(-1, 128)
    query_rows = query_up_store[0].reshape(-1, 128)
    pair_rows = key_value_store[0].reshape(-1, 128)
    n_down, n_query = down_rows.shape[0], query_rows.shape[0]
    n_row = n_down + n_query + pair_rows.shape[0]
    row = jnp.concatenate([down_rows, query_rows, pair_rows], axis=0)

    plane = gather_over(row, "ry", ny)
    blocks = jnp.stack([states] + [shifted(states, s, n_tp) for s in range(1, n_tp)])
    source = (tp_index - jnp.arange(n_tp, dtype=jnp.int32)) % n_tp
    piece = jnp.take(blocks, source, axis=0)
    plane_req = iz * ny + jnp.arange(ny, dtype=jnp.int32)

    slot_range = jnp.arange(n_req * store_rows, dtype=jnp.int32)
    used = jnp.any(slots_all[:, None] == slot_range[None, :], axis=0).astype(jnp.int32)
    prefix = jnp.sum(
        jnp.where(slot_range[None, :] < slot_range[:, None], used[None, :], 0), axis=1
    )

    per_column = ACTIVE // ny
    plane_slots = plane_req
    wanted = iy + ny * jnp.arange(per_column, dtype=jnp.int32)
    choose = (used[plane_slots][None, :] > 0) & (prefix[plane_slots][None, :] == wanted[:, None])
    column = jnp.sum(
        jnp.where(choose[:, :, None, None], plane[None], jnp.zeros((), plane.dtype)),
        axis=1,
    )
    column = spread_sum(column, "rz", nz)
    dest_k = prefix[slots_all[plane_req]]
    held = column[0]
    for m in range(1, per_column):
        held = jnp.where((dest_k // ny == m)[:, None, None], column[m], held)
    send = jnp.where((dest_k % ny == iy)[:, None, None], held, jnp.zeros((), held.dtype))
    received = lax.all_to_all(send, "ry", 0, 0, tiled=True)
    own_k = prefix[own_slot[0]]
    picked = received[own_k % ny]
    down_t = picked[:n_down].reshape(down_store.shape[2], down_store.shape[1])
    adapter_query = picked[n_down:n_down + n_query].reshape(query_up_store.shape[1:])
    adapter_pair = picked[n_down + n_query:].reshape(key_value_store.shape[1:])

    piece = jnp.transpose(piece, (1, 0, 2)).reshape(rows_total, -1)

    key_value_sum = jnp.dot(piece, key_value_weight, preferred_element_type=jnp.float32)

    rank_part = jnp.einsum("kd,sd->ks", down_t, states, preferred_element_type=jnp.float32)
    n_rank, width = rank_part.shape
    lanes = key_value_sum.shape[1]
    rank_rows = rank_part.reshape(-1, lanes)
    n_mid, n_up = rank_rows.shape[0], adapter_pair.shape[0]
    bundle = jnp.concatenate(
        [rank_rows, adapter_pair.astype(jnp.float32), key_value_sum], axis=0
    )
    arrived = gather_over(bundle, "tp", n_tp)
    rank_sum = arrived[0, :n_mid]
    for d in range(1, n_tp):
        rank_sum = rank_sum + arrived[d, :n_mid]
    rank_mid = rank_sum.reshape(n_rank, width).astype(jnp.bfloat16)
    rank_cols = rank_mid.shape[0] // 2
    up_all = arrived[:, n_mid:n_mid + n_up].astype(jnp.bfloat16)
    base_all = arrived[:, n_mid + n_up:]
    kv_heads = (n_tp * kv_cols) // 2 // HEAD_DIM
    group_index = tp_index * heads_here // (HEADS // kv_heads)
    key_up = up_all[group_index]
    value_up = up_all[kv_heads + group_index]
    key_sum = base_all[group_index]
    value_sum = base_all[kv_heads + group_index]

    query_total = jnp.dot(piece, query_weight, preferred_element_type=jnp.float32)
    query_addition = jnp.einsum(
        "ks,kc->sc", rank_mid[:rank_cols], adapter_query, preferred_element_type=jnp.float32
    )
    query_plain = query_total + adapter_scale * query_addition
    key_extra = jnp.einsum(
        "ks,kc->sc", rank_mid[rank_cols:], key_up, preferred_element_type=jnp.float32
    )
    value_extra = jnp.einsum(
        "ks,kc->sc", rank_mid[rank_cols:], value_up, preferred_element_type=jnp.float32
    )
    key_block = lax.reduce_precision(
        key_sum + adapter_scale * key_extra, exponent_bits=8, mantissa_bits=7
    )
    value_block = (value_sum + adapter_scale * value_extra).astype(jnp.bfloat16)

    queries = rotate(query_plain.reshape(req_dev, slot_len, heads_here, HEAD_DIM)).astype(
        jnp.bfloat16
    )
    keys_one = rotate(key_block.reshape(req_dev, slot_len, 1, HEAD_DIM)).astype(
        jnp.bfloat16
    )[:, :, 0, :]
    values_one = value_block.reshape(req_dev, slot_len, HEAD_DIM)
    scale = 1.0 / math.sqrt(HEAD_DIM)
    scores = (
        jnp.einsum("rqhd,rkd->rhqk", queries, keys_one, preferred_element_type=jnp.float32) * scale
    )
    position = jnp.arange(slot_len, dtype=jnp.int32)
    allowed = (position[None, None, :] <= position[None, :, None]) & (
        position[None, None, :] < lengths[:, None, None]
    )
    scores = jnp.where(allowed[:, None, :, :], scores, -jnp.inf)
    highest = jnp.max(scores, axis=-1, keepdims=True)
    expo = jnp.exp(scores - highest)
    weights = (expo / jnp.sum(expo, axis=-1, keepdims=True)).astype(jnp.bfloat16)
    context = jnp.einsum("rhqk,rkd->rqhd", weights, values_one, preferred_element_type=jnp.float32)
    live_rows = position[None, :] < lengths[:, None]
    context = jnp.where(live_rows[:, :, None, None], context, 0.0)
    return context.reshape(rows_total, q_cols).astype(jnp.bfloat16)


def solution(mesh):
    n_req = mesh.shape["req"]
    ny = 8 if n_req % 8 == 0 else 1
    split = jax.sharding.Mesh(
        mesh.devices.reshape(n_req // ny, ny, mesh.shape["tp"]), ("rz", "ry", "tp")
    )
    req = ("rz", "ry")
    return jax.shard_map(
        local,
        mesh=split,
        in_specs=(
            P(req, "tp"),
            P(None, "tp"),
            P(None, "tp"),
            P(req),
            P(req),
            P(),
            P(req, "tp", None),
            P(req, None, "tp"),
            P(req, None, "tp"),
        ),
        out_specs=P(req, "tp"),
        check_vma=False,
    )
```

```python
import math

import jax
import jax.numpy as jnp
from jax import lax
from jax.sharding import PartitionSpec as P

HEADS = 12
HEAD_DIM = 128
ACTIVE = 16


adapter_scale = 0.5
rope_base = 100000000000.0


def rotate(field):
    half = field.shape[-1] // 2
    count = field.shape[-3]
    position = jnp.arange(count).astype(jnp.float32)
    inverse = rope_base ** (-(jnp.arange(half).astype(jnp.float32) * 2.0) / field.shape[-1])
    angle = position[:, None] * inverse[None, :]
    cosine = jnp.cos(angle)[:, None, :]
    sine = jnp.sin(angle)[:, None, :]
    first_half = field[..., :half]
    second_half = field[..., half:]
    return jnp.concatenate(
        [first_half * cosine - second_half * sine, second_half * cosine + first_half * sine],
        axis=-1,
    )


def lookup_slots(wanted, adapter_slot):
    table = jnp.arange(adapter_slot.shape[0], dtype=jnp.int32)
    matches = wanted[:, None] == table[None, :]
    return jnp.sum(jnp.where(matches, adapter_slot[None, :], 0), axis=1)


def shifted(x, shift, n, pairs=None, axis="tp"):
    if pairs is None:
        pairs = [(i, (i + shift) % n) for i in range(n)]
    return lax.ppermute(x, axis, pairs)


def gather_over(x, axis, n):
    copies = jnp.broadcast_to(x[None], (n,) + x.shape)
    return lax.all_to_all(copies, axis, 0, 0, tiled=True)


def spread_sum(x, axis, n, radix=4):
    step = 1
    while step < n:
        width = min(radix, n // step)
        assert n % (step * width) == 0
        terms = [x] + [shifted(x, step * m, n, axis=axis) for m in range(1, width)]
        x = sum(terms[1:], terms[0])
        step *= width
    return x


def local(
    states,
    query_weight,
    key_value_weight,
    lengths,
    adapter_ids,
    adapter_slot,
    down_store,
    query_up_store,
    key_value_store,
):
    tp_index = lax.axis_index("tp")
    n_low = lax.axis_size("zl")
    iz = lax.axis_index("zh") * n_low + lax.axis_index("zl")
    iy = lax.axis_index("ry")
    n_tp = lax.axis_size("tp")
    nz = lax.axis_size("zh") * n_low
    ny = lax.axis_size("ry")
    n_req = nz * ny
    me = iz * ny + iy
    req_dev = lengths.shape[0]
    rows_total = states.shape[0]
    slot_len = rows_total // req_dev
    q_cols = query_weight.shape[1]
    kv_cols = key_value_weight.shape[1]
    heads_here = q_cols // HEAD_DIM
    store_rows = down_store.shape[0]
    assert req_dev == 1 and store_rows == 1 and ACTIVE % ny == 0

    own_slot = lookup_slots(adapter_ids, adapter_slot)

    slots_all = gather_over(own_slot, ("zh", "zl", "ry"), n_req).reshape(n_req)

    down_rows = down_store[0].T.reshape(-1, 128)
    query_rows = query_up_store[0].reshape(-1, 128)
    pair_rows = key_value_store[0].reshape(-1, 128)
    n_down, n_query = down_rows.shape[0], query_rows.shape[0]
    n_row = n_down + n_query + pair_rows.shape[0]
    row = jnp.concatenate([down_rows, query_rows, pair_rows], axis=0)

    plane = gather_over(row, "ry", ny)
    blocks = jnp.stack([states] + [shifted(states, s, n_tp) for s in range(1, n_tp)])
    source = (tp_index - jnp.arange(n_tp, dtype=jnp.int32)) % n_tp
    piece = jnp.take(blocks, source, axis=0)
    plane_req = iz * ny + jnp.arange(ny, dtype=jnp.int32)

    slot_range = jnp.arange(n_req * store_rows, dtype=jnp.int32)
    used = jnp.any(slots_all[:, None] == slot_range[None, :], axis=0).astype(jnp.int32)
    prefix = jnp.sum(
        jnp.where(slot_range[None, :] < slot_range[:, None], used[None, :], 0), axis=1
    )

    per_column = ACTIVE // ny
    plane_slots = plane_req
    wanted = iy + ny * jnp.arange(per_column, dtype=jnp.int32)
    choose = (used[plane_slots][None, :] > 0) & (prefix[plane_slots][None, :] == wanted[:, None])
    column = jnp.sum(
        jnp.where(choose[:, :, None, None], plane[None], jnp.zeros((), plane.dtype)),
        axis=1,
    )
    for axis in ("zl", "zh"):
        copies = gather_over(column, axis, lax.axis_size(axis))
        column = jnp.sum(copies, axis=0)
    dest_k = prefix[slots_all[plane_req]]
    held = column[0]
    for m in range(1, per_column):
        held = jnp.where((dest_k // ny == m)[:, None, None], column[m], held)
    send = jnp.where((dest_k % ny == iy)[:, None, None], held, jnp.zeros((), held.dtype))
    received = lax.all_to_all(send, "ry", 0, 0, tiled=True)
    own_k = prefix[own_slot[0]]
    picked = received[own_k % ny]
    down_t = picked[:n_down].reshape(down_store.shape[2], down_store.shape[1])
    adapter_query = picked[n_down:n_down + n_query].reshape(query_up_store.shape[1:])
    adapter_pair = picked[n_down + n_query:].reshape(key_value_store.shape[1:])

    piece = jnp.transpose(piece, (1, 0, 2)).reshape(rows_total, -1)

    key_value_sum = jnp.dot(piece, key_value_weight, preferred_element_type=jnp.float32)

    rank_part = jnp.einsum("kd,sd->ks", down_t, states, preferred_element_type=jnp.float32)
    n_rank, width = rank_part.shape
    lanes = key_value_sum.shape[1]
    rank_rows = rank_part.reshape(-1, lanes)
    n_mid, n_up = rank_rows.shape[0], adapter_pair.shape[0]
    bundle = jnp.concatenate(
        [rank_rows, adapter_pair.astype(jnp.float32), key_value_sum], axis=0
    )
    arrived = gather_over(bundle, "tp", n_tp)
    rank_sum = arrived[0, :n_mid]
    for d in range(1, n_tp):
        rank_sum = rank_sum + arrived[d, :n_mid]
    rank_mid = rank_sum.reshape(n_rank, width).astype(jnp.bfloat16)
    rank_cols = rank_mid.shape[0] // 2
    up_all = arrived[:, n_mid:n_mid + n_up].astype(jnp.bfloat16)
    base_all = arrived[:, n_mid + n_up:]
    kv_heads = (n_tp * kv_cols) // 2 // HEAD_DIM
    group_index = tp_index * heads_here // (HEADS // kv_heads)
    key_up = up_all[group_index]
    value_up = up_all[kv_heads + group_index]
    key_sum = base_all[group_index]
    value_sum = base_all[kv_heads + group_index]

    query_total = jnp.dot(piece, query_weight, preferred_element_type=jnp.float32)
    query_addition = jnp.einsum(
        "ks,kc->sc", rank_mid[:rank_cols], adapter_query, preferred_element_type=jnp.float32
    )
    query_plain = query_total + adapter_scale * query_addition
    key_extra = jnp.einsum(
        "ks,kc->sc", rank_mid[rank_cols:], key_up, preferred_element_type=jnp.float32
    )
    value_extra = jnp.einsum(
        "ks,kc->sc", rank_mid[rank_cols:], value_up, preferred_element_type=jnp.float32
    )
    key_block = lax.reduce_precision(
        key_sum + adapter_scale * key_extra, exponent_bits=8, mantissa_bits=7
    )
    value_block = (value_sum + adapter_scale * value_extra).astype(jnp.bfloat16)

    queries = rotate(query_plain.reshape(req_dev, slot_len, heads_here, HEAD_DIM)).astype(
        jnp.bfloat16
    )
    keys_one = rotate(key_block.reshape(req_dev, slot_len, 1, HEAD_DIM)).astype(
        jnp.bfloat16
    )[:, :, 0, :]
    values_one = value_block.reshape(req_dev, slot_len, HEAD_DIM)
    scale = 1.0 / math.sqrt(HEAD_DIM)
    scores = (
        jnp.einsum("rqhd,rkd->rhqk", queries, keys_one, preferred_element_type=jnp.float32) * scale
    )
    position = jnp.arange(slot_len, dtype=jnp.int32)
    allowed = (position[None, None, :] <= position[None, :, None]) & (
        position[None, None, :] < lengths[:, None, None]
    )
    scores = jnp.where(allowed[:, None, :, :], scores, -jnp.inf)
    highest = jnp.max(scores, axis=-1, keepdims=True)
    expo = jnp.exp(scores - highest)
    weights = (expo / jnp.sum(expo, axis=-1, keepdims=True)).astype(jnp.bfloat16)
    context = jnp.einsum("rhqk,rkd->rqhd", weights, values_one, preferred_element_type=jnp.float32)
    live_rows = position[None, :] < lengths[:, None]
    context = jnp.where(live_rows[:, :, None, None], context, 0.0)
    return context.reshape(rows_total, q_cols).astype(jnp.bfloat16)


def solution(mesh):
    n_req = mesh.shape["req"]
    ny = 8 if n_req % 8 == 0 else 1
    n_low = 4 if (n_req // ny) % 4 == 0 else 1
    split = jax.sharding.Mesh(
        mesh.devices.reshape(n_req // ny // n_low, n_low, ny, mesh.shape["tp"]),
        ("zh", "zl", "ry", "tp"),
    )
    req = ("zh", "zl", "ry")
    return jax.shard_map(
        local,
        mesh=split,
        in_specs=(
            P(req, "tp"),
            P(None, "tp"),
            P(None, "tp"),
            P(req),
            P(req),
            P(),
            P(req, "tp", None),
            P(req, None, "tp"),
            P(req, None, "tp"),
        ),
        out_specs=P(req, "tp"),
        check_vma=False,
    )
```

```python
import math

import jax
import jax.numpy as jnp
from jax import lax
from jax.sharding import PartitionSpec as P

HEADS = 12
HEAD_DIM = 128
ACTIVE = 16


adapter_scale = 0.5
rope_base = 100000000000.0


def rotate(field):
    half = field.shape[-1] // 2
    count = field.shape[-3]
    position = jnp.arange(count).astype(jnp.float32)
    inverse = rope_base ** (-(jnp.arange(half).astype(jnp.float32) * 2.0) / field.shape[-1])
    angle = position[:, None] * inverse[None, :]
    cosine = jnp.cos(angle)[:, None, :]
    sine = jnp.sin(angle)[:, None, :]
    first_half = field[..., :half]
    second_half = field[..., half:]
    return jnp.concatenate(
        [first_half * cosine - second_half * sine, second_half * cosine + first_half * sine],
        axis=-1,
    )


def lookup_slots(wanted, adapter_slot):
    table = jnp.arange(adapter_slot.shape[0], dtype=jnp.int32)
    matches = wanted[:, None] == table[None, :]
    return jnp.sum(jnp.where(matches, adapter_slot[None, :], 0), axis=1)


def shifted(x, shift, n, pairs=None, axis="tp"):
    if pairs is None:
        pairs = [(i, (i + shift) % n) for i in range(n)]
    return lax.ppermute(x, axis, pairs)


def gather_over(x, axis, n):
    copies = jnp.broadcast_to(x[None], (n,) + x.shape)
    return lax.all_to_all(copies, axis, 0, 0, tiled=True)


def spread_sum(x, axis, n, radix=4):
    step = 1
    while step < n:
        width = min(radix, n // step)
        assert n % (step * width) == 0
        terms = [x] + [shifted(x, step * m, n, axis=axis) for m in range(1, width)]
        x = sum(terms[1:], terms[0])
        step *= width
    return x


def local(
    states,
    query_weight,
    key_value_weight,
    lengths,
    adapter_ids,
    adapter_slot,
    down_store,
    query_up_store,
    key_value_store,
):
    tp_index = lax.axis_index("tp")
    n_low = lax.axis_size("zl")
    iz = lax.axis_index("zh") * n_low + lax.axis_index("zl")
    iy = lax.axis_index("ry")
    n_tp = lax.axis_size("tp")
    nz = lax.axis_size("zh") * n_low
    ny = lax.axis_size("ry")
    n_req = nz * ny
    me = iz * ny + iy
    req_dev = lengths.shape[0]
    rows_total = states.shape[0]
    slot_len = rows_total // req_dev
    q_cols = query_weight.shape[1]
    kv_cols = key_value_weight.shape[1]
    heads_here = q_cols // HEAD_DIM
    store_rows = down_store.shape[0]
    assert req_dev == 1 and store_rows == 1 and ACTIVE % ny == 0

    own_slot = lookup_slots(adapter_ids, adapter_slot)

    column_slots = gather_over(own_slot, "zl", n_low)
    column_slots = gather_over(column_slots, "zh", nz // n_low).reshape(nz)
    slots_all = gather_over(column_slots, "ry", ny).T.reshape(n_req)

    down_rows = down_store[0].T.reshape(-1, 128)
    query_rows = query_up_store[0].reshape(-1, 128)
    pair_rows = key_value_store[0].reshape(-1, 128)
    n_down, n_query = down_rows.shape[0], query_rows.shape[0]
    n_row = n_down + n_query + pair_rows.shape[0]
    row = jnp.concatenate([down_rows, query_rows, pair_rows], axis=0)

    plane = gather_over(row, "ry", ny)
    blocks = jnp.stack([states] + [shifted(states, s, n_tp) for s in range(1, n_tp)])
    source = (tp_index - jnp.arange(n_tp, dtype=jnp.int32)) % n_tp
    piece = jnp.take(blocks, source, axis=0)
    plane_req = iz * ny + jnp.arange(ny, dtype=jnp.int32)

    slot_range = jnp.arange(n_req * store_rows, dtype=jnp.int32)
    used = jnp.any(slots_all[:, None] == slot_range[None, :], axis=0).astype(jnp.int32)
    prefix = jnp.sum(
        jnp.where(slot_range[None, :] < slot_range[:, None], used[None, :], 0), axis=1
    )

    per_column = ACTIVE // ny
    plane_slots = plane_req
    wanted = iy + ny * jnp.arange(per_column, dtype=jnp.int32)
    choose = (used[plane_slots][None, :] > 0) & (prefix[plane_slots][None, :] == wanted[:, None])
    column = jnp.sum(
        jnp.where(choose[:, :, None, None], plane[None], jnp.zeros((), plane.dtype)),
        axis=1,
    )
    for axis in ("zl", "zh"):
        copies = gather_over(column, axis, lax.axis_size(axis))
        column = jnp.sum(copies, axis=0)
    dest_k = prefix[slots_all[plane_req]]
    held = column[0]
    for m in range(1, per_column):
        held = jnp.where((dest_k // ny == m)[:, None, None], column[m], held)
    send = jnp.where((dest_k % ny == iy)[:, None, None], held, jnp.zeros((), held.dtype))
    received = lax.all_to_all(send, "ry", 0, 0, tiled=True)
    own_k = prefix[own_slot[0]]
    picked = received[own_k % ny]
    down_t = picked[:n_down].reshape(down_store.shape[2], down_store.shape[1])
    adapter_query = picked[n_down:n_down + n_query].reshape(query_up_store.shape[1:])
    adapter_pair = picked[n_down + n_query:].reshape(key_value_store.shape[1:])

    piece = jnp.transpose(piece, (1, 0, 2)).reshape(rows_total, -1)

    key_value_sum = jnp.dot(piece, key_value_weight, preferred_element_type=jnp.float32)

    rank_part = jnp.einsum("kd,sd->ks", down_t, states, preferred_element_type=jnp.float32)
    n_rank, width = rank_part.shape
    lanes = key_value_sum.shape[1]
    rank_rows = rank_part.reshape(-1, lanes)
    n_mid, n_up = rank_rows.shape[0], adapter_pair.shape[0]
    bundle = jnp.concatenate(
        [rank_rows, adapter_pair.astype(jnp.float32), key_value_sum], axis=0
    )
    arrived = gather_over(bundle, "tp", n_tp)
    rank_sum = arrived[0, :n_mid]
    for d in range(1, n_tp):
        rank_sum = rank_sum + arrived[d, :n_mid]
    rank_mid = rank_sum.reshape(n_rank, width).astype(jnp.bfloat16)
    rank_cols = rank_mid.shape[0] // 2
    up_all = arrived[:, n_mid:n_mid + n_up].astype(jnp.bfloat16)
    base_all = arrived[:, n_mid + n_up:]
    kv_heads = (n_tp * kv_cols) // 2 // HEAD_DIM
    group_index = tp_index * heads_here // (HEADS // kv_heads)
    key_up = up_all[group_index]
    value_up = up_all[kv_heads + group_index]
    key_sum = base_all[group_index]
    value_sum = base_all[kv_heads + group_index]

    query_total = jnp.dot(piece, query_weight, preferred_element_type=jnp.float32)
    query_addition = jnp.einsum(
        "ks,kc->sc", rank_mid[:rank_cols], adapter_query, preferred_element_type=jnp.float32
    )
    query_plain = query_total + adapter_scale * query_addition
    key_extra = jnp.einsum(
        "ks,kc->sc", rank_mid[rank_cols:], key_up, preferred_element_type=jnp.float32
    )
    value_extra = jnp.einsum(
        "ks,kc->sc", rank_mid[rank_cols:], value_up, preferred_element_type=jnp.float32
    )
    key_block = lax.reduce_precision(
        key_sum + adapter_scale * key_extra, exponent_bits=8, mantissa_bits=7
    )
    value_block = (value_sum + adapter_scale * value_extra).astype(jnp.bfloat16)

    queries = rotate(query_plain.reshape(req_dev, slot_len, heads_here, HEAD_DIM)).astype(
        jnp.bfloat16
    )
    keys_one = rotate(key_block.reshape(req_dev, slot_len, 1, HEAD_DIM)).astype(
        jnp.bfloat16
    )[:, :, 0, :]
    values_one = value_block.reshape(req_dev, slot_len, HEAD_DIM)
    scale = 1.0 / math.sqrt(HEAD_DIM)
    scores = (
        jnp.einsum("rqhd,rkd->rhqk", queries, keys_one, preferred_element_type=jnp.float32) * scale
    )
    position = jnp.arange(slot_len, dtype=jnp.int32)
    allowed = (position[None, None, :] <= position[None, :, None]) & (
        position[None, None, :] < lengths[:, None, None]
    )
    scores = jnp.where(allowed[:, None, :, :], scores, -jnp.inf)
    highest = jnp.max(scores, axis=-1, keepdims=True)
    expo = jnp.exp(scores - highest)
    weights = (expo / jnp.sum(expo, axis=-1, keepdims=True)).astype(jnp.bfloat16)
    context = jnp.einsum("rhqk,rkd->rqhd", weights, values_one, preferred_element_type=jnp.float32)
    live_rows = position[None, :] < lengths[:, None]
    context = jnp.where(live_rows[:, :, None, None], context, 0.0)
    return context.reshape(rows_total, q_cols).astype(jnp.bfloat16)


def solution(mesh):
    n_req = mesh.shape["req"]
    ny = 8 if n_req % 8 == 0 else 1
    n_low = 4 if (n_req // ny) % 4 == 0 else 1
    split = jax.sharding.Mesh(
        mesh.devices.reshape(n_req // ny // n_low, n_low, ny, mesh.shape["tp"]),
        ("zh", "zl", "ry", "tp"),
    )
    req = ("zh", "zl", "ry")
    return jax.shard_map(
        local,
        mesh=split,
        in_specs=(
            P(req, "tp"),
            P(None, "tp"),
            P(None, "tp"),
            P(req),
            P(req),
            P(),
            P(req, "tp", None),
            P(req, None, "tp"),
            P(req, None, "tp"),
        ),
        out_specs=P(req, "tp"),
        check_vma=False,
    )
```

```python
import math

import jax
import jax.numpy as jnp
from jax import lax
from jax.sharding import PartitionSpec as P

HEADS = 12
HEAD_DIM = 128
ACTIVE = 16


adapter_scale = 0.5
rope_base = 100000000000.0


def rotate(field):
    half = field.shape[-1] // 2
    count = field.shape[-3]
    position = jnp.arange(count).astype(jnp.float32)
    inverse = rope_base ** (-(jnp.arange(half).astype(jnp.float32) * 2.0) / field.shape[-1])
    angle = position[:, None] * inverse[None, :]
    cosine = jnp.cos(angle)[:, None, :]
    sine = jnp.sin(angle)[:, None, :]
    first_half = field[..., :half]
    second_half = field[..., half:]
    return jnp.concatenate(
        [first_half * cosine - second_half * sine, second_half * cosine + first_half * sine],
        axis=-1,
    )


def lookup_slots(wanted, adapter_slot):
    table = jnp.arange(adapter_slot.shape[0], dtype=jnp.int32)
    matches = wanted[:, None] == table[None, :]
    return jnp.sum(jnp.where(matches, adapter_slot[None, :], 0), axis=1)


def shifted(x, shift, n, pairs=None, axis="tp"):
    if pairs is None:
        pairs = [(i, (i + shift) % n) for i in range(n)]
    return lax.ppermute(x, axis, pairs)


def gather_over(x, axis, n):
    copies = jnp.broadcast_to(x[None], (n,) + x.shape)
    return lax.all_to_all(copies, axis, 0, 0, tiled=True)


def spread_sum(x, axis, n, radix=4):
    step = 1
    while step < n:
        width = min(radix, n // step)
        assert n % (step * width) == 0
        terms = [x] + [shifted(x, step * m, n, axis=axis) for m in range(1, width)]
        x = sum(terms[1:], terms[0])
        step *= width
    return x


def local(
    states,
    query_weight,
    key_value_weight,
    lengths,
    adapter_ids,
    adapter_slot,
    down_store,
    query_up_store,
    key_value_store,
):
    tp_index = lax.axis_index("tp")
    n_low = lax.axis_size("zl")
    iz = lax.axis_index("zh") * n_low + lax.axis_index("zl")
    iy = lax.axis_index("ry")
    n_tp = lax.axis_size("tp")
    nz = lax.axis_size("zh") * n_low
    ny = lax.axis_size("ry")
    n_req = nz * ny
    me = iz * ny + iy
    req_dev = lengths.shape[0]
    rows_total = states.shape[0]
    slot_len = rows_total // req_dev
    q_cols = query_weight.shape[1]
    kv_cols = key_value_weight.shape[1]
    heads_here = q_cols // HEAD_DIM
    store_rows = down_store.shape[0]
    assert req_dev == 1 and store_rows == 1 and ACTIVE % ny == 0

    own_slot = lookup_slots(adapter_ids, adapter_slot)

    slots_all = gather_over(own_slot, ("zh", "zl", "ry"), n_req).reshape(n_req)

    down_rows = down_store[0].T.reshape(-1, 128)
    query_rows = query_up_store[0].reshape(-1, 128)
    pair_rows = key_value_store[0].reshape(-1, 128)
    n_down, n_query = down_rows.shape[0], query_rows.shape[0]
    n_row = n_down + n_query + pair_rows.shape[0]
    row = jnp.concatenate([down_rows, query_rows, pair_rows], axis=0)

    plane = jnp.stack([row] + [shifted(row, s, ny, axis="ry") for s in range(1, ny)])
    blocks = jnp.stack([states] + [shifted(states, s, n_tp) for s in range(1, n_tp)])
    source = (tp_index - jnp.arange(n_tp, dtype=jnp.int32)) % n_tp
    piece = jnp.take(blocks, source, axis=0)
    plane_req = iz * ny + (iy - jnp.arange(ny, dtype=jnp.int32)) % ny

    slot_range = jnp.arange(n_req * store_rows, dtype=jnp.int32)
    used = jnp.any(slots_all[:, None] == slot_range[None, :], axis=0).astype(jnp.int32)
    prefix = jnp.sum(
        jnp.where(slot_range[None, :] < slot_range[:, None], used[None, :], 0), axis=1
    )

    per_column = ACTIVE // ny
    plane_slots = plane_req
    wanted = iy + ny * jnp.arange(per_column, dtype=jnp.int32)
    choose = (used[plane_slots][None, :] > 0) & (prefix[plane_slots][None, :] == wanted[:, None])
    column = jnp.sum(
        jnp.where(choose[:, :, None, None], plane[None], jnp.zeros((), plane.dtype)),
        axis=1,
    )
    for axis in ("zl", "zh"):
        copies = gather_over(column, axis, lax.axis_size(axis))
        column = jnp.sum(copies, axis=0)
    dest_k = prefix[slots_all[iz * ny + jnp.arange(ny, dtype=jnp.int32)]]
    held = column[0]
    for m in range(1, per_column):
        held = jnp.where((dest_k // ny == m)[:, None, None], column[m], held)
    send = jnp.where((dest_k % ny == iy)[:, None, None], held, jnp.zeros((), held.dtype))
    received = lax.all_to_all(send, "ry", 0, 0, tiled=True)
    own_k = prefix[own_slot[0]]
    picked = received[own_k % ny]
    down_t = picked[:n_down].reshape(down_store.shape[2], down_store.shape[1])
    adapter_query = picked[n_down:n_down + n_query].reshape(query_up_store.shape[1:])
    adapter_pair = picked[n_down + n_query:].reshape(key_value_store.shape[1:])

    piece = jnp.transpose(piece, (1, 0, 2)).reshape(rows_total, -1)

    key_value_sum = jnp.dot(piece, key_value_weight, preferred_element_type=jnp.float32)

    rank_part = jnp.einsum("kd,sd->ks", down_t, states, preferred_element_type=jnp.float32)
    n_rank, width = rank_part.shape
    lanes = key_value_sum.shape[1]
    rank_rows = rank_part.reshape(-1, lanes)
    n_mid, n_up = rank_rows.shape[0], adapter_pair.shape[0]
    bundle = jnp.concatenate(
        [rank_rows, adapter_pair.astype(jnp.float32), key_value_sum], axis=0
    )
    arrived = gather_over(bundle, "tp", n_tp)
    rank_sum = arrived[0, :n_mid]
    for d in range(1, n_tp):
        rank_sum = rank_sum + arrived[d, :n_mid]
    rank_mid = rank_sum.reshape(n_rank, width).astype(jnp.bfloat16)
    rank_cols = rank_mid.shape[0] // 2
    up_all = arrived[:, n_mid:n_mid + n_up].astype(jnp.bfloat16)
    base_all = arrived[:, n_mid + n_up:]
    kv_heads = (n_tp * kv_cols) // 2 // HEAD_DIM
    group_index = tp_index * heads_here // (HEADS // kv_heads)
    key_up = up_all[group_index]
    value_up = up_all[kv_heads + group_index]
    key_sum = base_all[group_index]
    value_sum = base_all[kv_heads + group_index]

    query_total = jnp.dot(piece, query_weight, preferred_element_type=jnp.float32)
    query_addition = jnp.einsum(
        "ks,kc->sc", rank_mid[:rank_cols], adapter_query, preferred_element_type=jnp.float32
    )
    query_plain = query_total + adapter_scale * query_addition
    key_extra = jnp.einsum(
        "ks,kc->sc", rank_mid[rank_cols:], key_up, preferred_element_type=jnp.float32
    )
    value_extra = jnp.einsum(
        "ks,kc->sc", rank_mid[rank_cols:], value_up, preferred_element_type=jnp.float32
    )
    key_block = lax.reduce_precision(
        key_sum + adapter_scale * key_extra, exponent_bits=8, mantissa_bits=7
    )
    value_block = (value_sum + adapter_scale * value_extra).astype(jnp.bfloat16)

    queries = rotate(query_plain.reshape(req_dev, slot_len, heads_here, HEAD_DIM)).astype(
        jnp.bfloat16
    )
    keys_one = rotate(key_block.reshape(req_dev, slot_len, 1, HEAD_DIM)).astype(
        jnp.bfloat16
    )[:, :, 0, :]
    values_one = value_block.reshape(req_dev, slot_len, HEAD_DIM)
    scale = 1.0 / math.sqrt(HEAD_DIM)
    scores = (
        jnp.einsum("rqhd,rkd->rhqk", queries, keys_one, preferred_element_type=jnp.float32) * scale
    )
    position = jnp.arange(slot_len, dtype=jnp.int32)
    allowed = (position[None, None, :] <= position[None, :, None]) & (
        position[None, None, :] < lengths[:, None, None]
    )
    scores = jnp.where(allowed[:, None, :, :], scores, -jnp.inf)
    highest = jnp.max(scores, axis=-1, keepdims=True)
    expo = jnp.exp(scores - highest)
    weights = (expo / jnp.sum(expo, axis=-1, keepdims=True)).astype(jnp.bfloat16)
    context = jnp.einsum("rhqk,rkd->rqhd", weights, values_one, preferred_element_type=jnp.float32)
    live_rows = position[None, :] < lengths[:, None]
    context = jnp.where(live_rows[:, :, None, None], context, 0.0)
    return context.reshape(rows_total, q_cols).astype(jnp.bfloat16)


def solution(mesh):
    n_req = mesh.shape["req"]
    ny = 8 if n_req % 8 == 0 else 1
    n_low = 4 if (n_req // ny) % 4 == 0 else 1
    split = jax.sharding.Mesh(
        mesh.devices.reshape(n_req // ny // n_low, n_low, ny, mesh.shape["tp"]),
        ("zh", "zl", "ry", "tp"),
    )
    req = ("zh", "zl", "ry")
    return jax.shard_map(
        local,
        mesh=split,
        in_specs=(
            P(req, "tp"),
            P(None, "tp"),
            P(None, "tp"),
            P(req),
            P(req),
            P(),
            P(req, "tp", None),
            P(req, None, "tp"),
            P(req, None, "tp"),
        ),
        out_specs=P(req, "tp"),
        check_vma=False,
    )
```

```python
import math

import jax
import jax.numpy as jnp
from jax import lax
from jax.sharding import PartitionSpec as P

HEADS = 12
HEAD_DIM = 128
ACTIVE = 16


adapter_scale = 0.5
rope_base = 100000000000.0


def rotate(field):
    half = field.shape[-1] // 2
    count = field.shape[-3]
    position = jnp.arange(count).astype(jnp.float32)
    inverse = rope_base ** (-(jnp.arange(half).astype(jnp.float32) * 2.0) / field.shape[-1])
    angle = position[:, None] * inverse[None, :]
    cosine = jnp.cos(angle)[:, None, :]
    sine = jnp.sin(angle)[:, None, :]
    first_half = field[..., :half]
    second_half = field[..., half:]
    return jnp.concatenate(
        [first_half * cosine - second_half * sine, second_half * cosine + first_half * sine],
        axis=-1,
    )


def lookup_slots(wanted, adapter_slot):
    table = jnp.arange(adapter_slot.shape[0], dtype=jnp.int32)
    matches = wanted[:, None] == table[None, :]
    return jnp.sum(jnp.where(matches, adapter_slot[None, :], 0), axis=1)


def shifted(x, shift, n, pairs=None, axis="tp"):
    if pairs is None:
        pairs = [(i, (i + shift) % n) for i in range(n)]
    return lax.ppermute(x, axis, pairs)


def gather_over(x, axis, n):
    copies = jnp.broadcast_to(x[None], (n,) + x.shape)
    return lax.all_to_all(copies, axis, 0, 0, tiled=True)


def spread_sum(x, axis, n, radix=4):
    step = 1
    while step < n:
        width = min(radix, n // step)
        assert n % (step * width) == 0
        terms = [x] + [shifted(x, step * m, n, axis=axis) for m in range(1, width)]
        x = sum(terms[1:], terms[0])
        step *= width
    return x


def local(
    states,
    query_weight,
    key_value_weight,
    lengths,
    adapter_ids,
    adapter_slot,
    down_store,
    query_up_store,
    key_value_store,
):
    tp_index = lax.axis_index("tp")
    n_low = lax.axis_size("zl")
    iz = lax.axis_index("zh") * n_low + lax.axis_index("zl")
    iy = lax.axis_index("ry")
    n_tp = lax.axis_size("tp")
    nz = lax.axis_size("zh") * n_low
    ny = lax.axis_size("ry")
    n_req = nz * ny
    me = iz * ny + iy
    req_dev = lengths.shape[0]
    rows_total = states.shape[0]
    slot_len = rows_total // req_dev
    q_cols = query_weight.shape[1]
    kv_cols = key_value_weight.shape[1]
    heads_here = q_cols // HEAD_DIM
    store_rows = down_store.shape[0]
    assert req_dev == 1 and store_rows == 1 and ACTIVE % ny == 0

    own_slot = lookup_slots(adapter_ids, adapter_slot)

    slots_all = gather_over(own_slot, ("zh", "zl", "ry"), n_req).reshape(n_req)

    down_rows = down_store[0].T.reshape(-1, 128)
    query_rows = query_up_store[0].reshape(-1, 128)
    pair_rows = key_value_store[0].reshape(-1, 128)
    n_down, n_query = down_rows.shape[0], query_rows.shape[0]
    n_row = n_down + n_query + pair_rows.shape[0]
    row = jnp.concatenate([down_rows, query_rows, pair_rows], axis=0)

    plane = gather_over(row, "ry", ny)
    blocks = jnp.stack([states] + [shifted(states, s, n_tp) for s in range(1, n_tp)])
    source = (tp_index - jnp.arange(n_tp, dtype=jnp.int32)) % n_tp
    piece = jnp.take(blocks, source, axis=0)
    plane_req = iz * ny + jnp.arange(ny, dtype=jnp.int32)

    slot_range = jnp.arange(n_req * store_rows, dtype=jnp.int32)
    used = jnp.any(slots_all[:, None] == slot_range[None, :], axis=0).astype(jnp.int32)
    prefix = jnp.sum(
        jnp.where(slot_range[None, :] < slot_range[:, None], used[None, :], 0), axis=1
    )

    per_column = ACTIVE // ny
    plane_slots = plane_req
    wanted = iy + ny * jnp.arange(per_column, dtype=jnp.int32)
    choose = (used[plane_slots][None, :] > 0) & (prefix[plane_slots][None, :] == wanted[:, None])
    column = jnp.sum(
        jnp.where(choose[:, :, None, None], plane[None], jnp.zeros((), plane.dtype)),
        axis=1,
    )
    for axis in ("zl", "zh"):
        copies = gather_over(column, axis, lax.axis_size(axis))
        column = jnp.sum(copies, axis=0)
    dest_k = prefix[slots_all[plane_req]]
    held = column[0]
    for m in range(1, per_column):
        held = jnp.where((dest_k // ny == m)[:, None, None], column[m], held)
    send = jnp.where((dest_k % ny == iy)[:, None, None], held, jnp.zeros((), held.dtype))
    received = lax.all_to_all(send, "ry", 0, 0, tiled=True)
    own_k = prefix[own_slot[0]]
    picked = received[own_k % ny]
    down_t = picked[:n_down].reshape(down_store.shape[2], down_store.shape[1])
    adapter_query = picked[n_down:n_down + n_query].reshape(query_up_store.shape[1:])
    adapter_pair = picked[n_down + n_query:].reshape(key_value_store.shape[1:])

    piece = jnp.transpose(piece, (1, 0, 2)).reshape(rows_total, -1)

    key_value_sum = jnp.dot(piece, key_value_weight, preferred_element_type=jnp.float32)
    from_left = shifted(key_value_sum, 1, n_tp, [(0, 1), (1, 2)])
    from_right = shifted(key_value_sum, -1, n_tp, [(2, 1), (3, 2)])
    from_far = shifted(key_value_sum, 2, n_tp, [(1, 3), (2, 0)])
    key_sum = jnp.where(
        tp_index == 0, key_value_sum, jnp.where(tp_index == 3, from_far, from_left)
    )
    value_sum = jnp.where(
        tp_index == 3, key_value_sum, jnp.where(tp_index == 0, from_far, from_right)
    )

    rank_part = jnp.einsum("kd,sd->ks", down_t, states, preferred_element_type=jnp.float32)
    n_rank, width = rank_part.shape
    lanes = key_value_sum.shape[1]
    rank_rows = rank_part.reshape(-1, lanes)
    n_mid, n_up = rank_rows.shape[0], adapter_pair.shape[0]
    bundle = jnp.concatenate(
        [rank_rows, adapter_pair.astype(jnp.float32)], axis=0
    )
    arrived = gather_over(bundle, "tp", n_tp)
    rank_sum = arrived[0, :n_mid]
    for d in range(1, n_tp):
        rank_sum = rank_sum + arrived[d, :n_mid]
    rank_mid = rank_sum.reshape(n_rank, width).astype(jnp.bfloat16)
    rank_cols = rank_mid.shape[0] // 2
    up_all = arrived[:, n_mid:n_mid + n_up].astype(jnp.bfloat16)
    kv_heads = (n_tp * kv_cols) // 2 // HEAD_DIM
    group_index = tp_index * heads_here // (HEADS // kv_heads)
    key_up = up_all[group_index]
    value_up = up_all[kv_heads + group_index]

    query_total = jnp.dot(piece, query_weight, preferred_element_type=jnp.float32)
    query_addition = jnp.einsum(
        "ks,kc->sc", rank_mid[:rank_cols], adapter_query, preferred_element_type=jnp.float32
    )
    query_plain = query_total + adapter_scale * query_addition
    key_extra = jnp.einsum(
        "ks,kc->sc", rank_mid[rank_cols:], key_up, preferred_element_type=jnp.float32
    )
    value_extra = jnp.einsum(
        "ks,kc->sc", rank_mid[rank_cols:], value_up, preferred_element_type=jnp.float32
    )
    key_block = lax.reduce_precision(
        key_sum + adapter_scale * key_extra, exponent_bits=8, mantissa_bits=7
    )
    value_block = (value_sum + adapter_scale * value_extra).astype(jnp.bfloat16)

    queries = rotate(query_plain.reshape(req_dev, slot_len, heads_here, HEAD_DIM)).astype(
        jnp.bfloat16
    )
    keys_one = rotate(key_block.reshape(req_dev, slot_len, 1, HEAD_DIM)).astype(
        jnp.bfloat16
    )[:, :, 0, :]
    values_one = value_block.reshape(req_dev, slot_len, HEAD_DIM)
    scale = 1.0 / math.sqrt(HEAD_DIM)
    scores = (
        jnp.einsum("rqhd,rkd->rhqk", queries, keys_one, preferred_element_type=jnp.float32) * scale
    )
    position = jnp.arange(slot_len, dtype=jnp.int32)
    allowed = (position[None, None, :] <= position[None, :, None]) & (
        position[None, None, :] < lengths[:, None, None]
    )
    scores = jnp.where(allowed[:, None, :, :], scores, -jnp.inf)
    highest = jnp.max(scores, axis=-1, keepdims=True)
    expo = jnp.exp(scores - highest)
    weights = (expo / jnp.sum(expo, axis=-1, keepdims=True)).astype(jnp.bfloat16)
    context = jnp.einsum("rhqk,rkd->rqhd", weights, values_one, preferred_element_type=jnp.float32)
    live_rows = position[None, :] < lengths[:, None]
    context = jnp.where(live_rows[:, :, None, None], context, 0.0)
    return context.reshape(rows_total, q_cols).astype(jnp.bfloat16)


def solution(mesh):
    n_req = mesh.shape["req"]
    ny = 8 if n_req % 8 == 0 else 1
    n_low = 4 if (n_req // ny) % 4 == 0 else 1
    split = jax.sharding.Mesh(
        mesh.devices.reshape(n_req // ny // n_low, n_low, ny, mesh.shape["tp"]),
        ("zh", "zl", "ry", "tp"),
    )
    req = ("zh", "zl", "ry")
    return jax.shard_map(
        local,
        mesh=split,
        in_specs=(
            P(req, "tp"),
            P(None, "tp"),
            P(None, "tp"),
            P(req),
            P(req),
            P(),
            P(req, "tp", None),
            P(req, None, "tp"),
            P(req, None, "tp"),
        ),
        out_specs=P(req, "tp"),
        check_vma=False,
    )
```

```python
import math

import jax
import jax.numpy as jnp
from jax import lax
from jax.sharding import PartitionSpec as P

HEADS = 12
HEAD_DIM = 128
ACTIVE = 16


adapter_scale = 0.5
rope_base = 100000000000.0


def rotate(field):
    half = field.shape[-1] // 2
    count = field.shape[-3]
    position = jnp.arange(count).astype(jnp.float32)
    inverse = rope_base ** (-(jnp.arange(half).astype(jnp.float32) * 2.0) / field.shape[-1])
    angle = position[:, None] * inverse[None, :]
    cosine = jnp.cos(angle)[:, None, :]
    sine = jnp.sin(angle)[:, None, :]
    first_half = field[..., :half]
    second_half = field[..., half:]
    return jnp.concatenate(
        [first_half * cosine - second_half * sine, second_half * cosine + first_half * sine],
        axis=-1,
    )


def lookup_slots(wanted, adapter_slot):
    table = jnp.arange(adapter_slot.shape[0], dtype=jnp.int32)
    matches = wanted[:, None] == table[None, :]
    return jnp.sum(jnp.where(matches, adapter_slot[None, :], 0), axis=1)


def shifted(x, shift, n, pairs=None, axis="tp"):
    if pairs is None:
        pairs = [(i, (i + shift) % n) for i in range(n)]
    return lax.ppermute(x, axis, pairs)


def gather_over(x, axis, n):
    copies = jnp.broadcast_to(x[None], (n,) + x.shape)
    return lax.all_to_all(copies, axis, 0, 0, tiled=True)


def spread_sum(x, axis, n, radix=4):
    step = 1
    while step < n:
        width = min(radix, n // step)
        assert n % (step * width) == 0
        terms = [x] + [shifted(x, step * m, n, axis=axis) for m in range(1, width)]
        x = sum(terms[1:], terms[0])
        step *= width
    return x


def local(
    states,
    query_weight,
    key_value_weight,
    lengths,
    adapter_ids,
    adapter_slot,
    down_store,
    query_up_store,
    key_value_store,
):
    tp_index = lax.axis_index("tp")
    n_low = lax.axis_size("zl")
    iz = lax.axis_index("zh") * n_low + lax.axis_index("zl")
    iy = lax.axis_index("ry")
    n_tp = lax.axis_size("tp")
    nz = lax.axis_size("zh") * n_low
    ny = lax.axis_size("ry")
    n_req = nz * ny
    me = iz * ny + iy
    req_dev = lengths.shape[0]
    rows_total = states.shape[0]
    slot_len = rows_total // req_dev
    q_cols = query_weight.shape[1]
    kv_cols = key_value_weight.shape[1]
    heads_here = q_cols // HEAD_DIM
    store_rows = down_store.shape[0]
    assert req_dev == 1 and store_rows == 1 and ACTIVE % ny == 0

    own_slot = lookup_slots(adapter_ids, adapter_slot)

    slots_all = gather_over(own_slot, ("zh", "zl", "ry"), n_req).reshape(n_req)

    down_rows = down_store[0].T.reshape(-1, 128)
    query_rows = query_up_store[0].reshape(-1, 128)
    pair_rows = key_value_store[0].reshape(-1, 128)
    n_down, n_query = down_rows.shape[0], query_rows.shape[0]
    n_row = n_down + n_query + pair_rows.shape[0]
    row = jnp.concatenate([down_rows, query_rows, pair_rows], axis=0)

    plane = gather_over(row, "ry", ny)
    blocks = jnp.stack([states] + [shifted(states, s, n_tp) for s in range(1, n_tp)])
    source = (tp_index - jnp.arange(n_tp, dtype=jnp.int32)) % n_tp
    piece = jnp.take(blocks, source, axis=0)
    plane_req = iz * ny + jnp.arange(ny, dtype=jnp.int32)

    slot_range = jnp.arange(n_req * store_rows, dtype=jnp.int32)
    used = jnp.any(slots_all[:, None] == slot_range[None, :], axis=0).astype(jnp.int32)
    prefix = jnp.sum(
        jnp.where(slot_range[None, :] < slot_range[:, None], used[None, :], 0), axis=1
    )

    per_column = ACTIVE // ny
    plane_slots = plane_req
    wanted = iy + ny * jnp.arange(per_column, dtype=jnp.int32)
    choose = (used[plane_slots][None, :] > 0) & (prefix[plane_slots][None, :] == wanted[:, None])
    column = jnp.sum(
        jnp.where(choose[:, :, None, None], plane[None], jnp.zeros((), plane.dtype)),
        axis=1,
    )
    for axis in ("zh", "zl"):
        copies = gather_over(column, axis, lax.axis_size(axis))
        column = jnp.sum(copies, axis=0)
    dest_k = prefix[slots_all[plane_req]]
    held = column[0]
    for m in range(1, per_column):
        held = jnp.where((dest_k // ny == m)[:, None, None], column[m], held)
    send = jnp.where((dest_k % ny == iy)[:, None, None], held, jnp.zeros((), held.dtype))
    received = lax.all_to_all(send, "ry", 0, 0, tiled=True)
    own_k = prefix[own_slot[0]]
    picked = received[own_k % ny]
    down_t = picked[:n_down].reshape(down_store.shape[2], down_store.shape[1])
    adapter_query = picked[n_down:n_down + n_query].reshape(query_up_store.shape[1:])
    adapter_pair = picked[n_down + n_query:].reshape(key_value_store.shape[1:])

    piece = jnp.transpose(piece, (1, 0, 2)).reshape(rows_total, -1)

    key_value_sum = jnp.dot(piece, key_value_weight, preferred_element_type=jnp.float32)
    from_left = shifted(key_value_sum, 1, n_tp, [(0, 1), (1, 2)])
    from_right = shifted(key_value_sum, -1, n_tp, [(2, 1), (3, 2)])
    from_far = shifted(key_value_sum, 2, n_tp, [(1, 3), (2, 0)])
    key_sum = jnp.where(
        tp_index == 0, key_value_sum, jnp.where(tp_index == 3, from_far, from_left)
    )
    value_sum = jnp.where(
        tp_index == 3, key_value_sum, jnp.where(tp_index == 0, from_far, from_right)
    )

    rank_part = jnp.einsum("kd,sd->ks", down_t, states, preferred_element_type=jnp.float32)
    n_rank, width = rank_part.shape
    lanes = key_value_sum.shape[1]
    rank_rows = rank_part.reshape(-1, lanes)
    n_mid, n_up = rank_rows.shape[0], adapter_pair.shape[0]
    bundle = jnp.concatenate(
        [rank_rows, adapter_pair.astype(jnp.float32)], axis=0
    )
    arrived = gather_over(bundle, "tp", n_tp)
    rank_sum = arrived[0, :n_mid]
    for d in range(1, n_tp):
        rank_sum = rank_sum + arrived[d, :n_mid]
    rank_mid = rank_sum.reshape(n_rank, width).astype(jnp.bfloat16)
    rank_cols = rank_mid.shape[0] // 2
    up_all = arrived[:, n_mid:n_mid + n_up].astype(jnp.bfloat16)
    kv_heads = (n_tp * kv_cols) // 2 // HEAD_DIM
    group_index = tp_index * heads_here // (HEADS // kv_heads)
    key_up = up_all[group_index]
    value_up = up_all[kv_heads + group_index]

    query_total = jnp.dot(piece, query_weight, preferred_element_type=jnp.float32)
    query_addition = jnp.einsum(
        "ks,kc->sc", rank_mid[:rank_cols], adapter_query, preferred_element_type=jnp.float32
    )
    query_plain = query_total + adapter_scale * query_addition
    key_extra = jnp.einsum(
        "ks,kc->sc", rank_mid[rank_cols:], key_up, preferred_element_type=jnp.float32
    )
    value_extra = jnp.einsum(
        "ks,kc->sc", rank_mid[rank_cols:], value_up, preferred_element_type=jnp.float32
    )
    key_block = lax.reduce_precision(
        key_sum + adapter_scale * key_extra, exponent_bits=8, mantissa_bits=7
    )
    value_block = (value_sum + adapter_scale * value_extra).astype(jnp.bfloat16)

    queries = rotate(query_plain.reshape(req_dev, slot_len, heads_here, HEAD_DIM)).astype(
        jnp.bfloat16
    )
    keys_one = rotate(key_block.reshape(req_dev, slot_len, 1, HEAD_DIM)).astype(
        jnp.bfloat16
    )[:, :, 0, :]
    values_one = value_block.reshape(req_dev, slot_len, HEAD_DIM)
    scale = 1.0 / math.sqrt(HEAD_DIM)
    scores = (
        jnp.einsum("rqhd,rkd->rhqk", queries, keys_one, preferred_element_type=jnp.float32) * scale
    )
    position = jnp.arange(slot_len, dtype=jnp.int32)
    allowed = (position[None, None, :] <= position[None, :, None]) & (
        position[None, None, :] < lengths[:, None, None]
    )
    scores = jnp.where(allowed[:, None, :, :], scores, -jnp.inf)
    highest = jnp.max(scores, axis=-1, keepdims=True)
    expo = jnp.exp(scores - highest)
    weights = (expo / jnp.sum(expo, axis=-1, keepdims=True)).astype(jnp.bfloat16)
    context = jnp.einsum("rhqk,rkd->rqhd", weights, values_one, preferred_element_type=jnp.float32)
    live_rows = position[None, :] < lengths[:, None]
    context = jnp.where(live_rows[:, :, None, None], context, 0.0)
    return context.reshape(rows_total, q_cols).astype(jnp.bfloat16)


def solution(mesh):
    n_req = mesh.shape["req"]
    ny = 8 if n_req % 8 == 0 else 1
    n_low = 4 if (n_req // ny) % 4 == 0 else 1
    split = jax.sharding.Mesh(
        mesh.devices.reshape(n_req // ny // n_low, n_low, ny, mesh.shape["tp"]),
        ("zh", "zl", "ry", "tp"),
    )
    req = ("zh", "zl", "ry")
    return jax.shard_map(
        local,
        mesh=split,
        in_specs=(
            P(req, "tp"),
            P(None, "tp"),
            P(None, "tp"),
            P(req),
            P(req),
            P(),
            P(req, "tp", None),
            P(req, None, "tp"),
            P(req, None, "tp"),
        ),
        out_specs=P(req, "tp"),
        check_vma=False,
    )
```

```python
import math

import jax
import jax.numpy as jnp
from jax import lax
from jax.sharding import PartitionSpec as P

HEADS = 12
HEAD_DIM = 128
ACTIVE = 16


adapter_scale = 0.5
rope_base = 100000000000.0


def rotate(field):
    half = field.shape[-1] // 2
    count = field.shape[-3]
    position = jnp.arange(count).astype(jnp.float32)
    inverse = rope_base ** (-(jnp.arange(half).astype(jnp.float32) * 2.0) / field.shape[-1])
    angle = position[:, None] * inverse[None, :]
    cosine = jnp.cos(angle)[:, None, :]
    sine = jnp.sin(angle)[:, None, :]
    first_half = field[..., :half]
    second_half = field[..., half:]
    return jnp.concatenate(
        [first_half * cosine - second_half * sine, second_half * cosine + first_half * sine],
        axis=-1,
    )


def lookup_slots(wanted, adapter_slot):
    table = jnp.arange(adapter_slot.shape[0], dtype=jnp.int32)
    matches = wanted[:, None] == table[None, :]
    return jnp.sum(jnp.where(matches, adapter_slot[None, :], 0), axis=1)


def shifted(x, shift, n, pairs=None, axis="tp"):
    if pairs is None:
        pairs = [(i, (i + shift) % n) for i in range(n)]
    return lax.ppermute(x, axis, pairs)


def gather_over(x, axis, n):
    copies = jnp.broadcast_to(x[None], (n,) + x.shape)
    return lax.all_to_all(copies, axis, 0, 0, tiled=True)


def spread_sum(x, axis, n, radix=4):
    step = 1
    while step < n:
        width = min(radix, n // step)
        assert n % (step * width) == 0
        terms = [x] + [shifted(x, step * m, n, axis=axis) for m in range(1, width)]
        x = sum(terms[1:], terms[0])
        step *= width
    return x


def local(
    states,
    query_weight,
    key_value_weight,
    lengths,
    adapter_ids,
    adapter_slot,
    down_store,
    query_up_store,
    key_value_store,
):
    tp_index = lax.axis_index("tp")
    n_low = lax.axis_size("zl")
    iz = lax.axis_index("zh") * n_low + lax.axis_index("zl")
    iy = lax.axis_index("ry")
    n_tp = lax.axis_size("tp")
    nz = lax.axis_size("zh") * n_low
    ny = lax.axis_size("ry")
    n_req = nz * ny
    me = iz * ny + iy
    req_dev = lengths.shape[0]
    rows_total = states.shape[0]
    slot_len = rows_total // req_dev
    q_cols = query_weight.shape[1]
    kv_cols = key_value_weight.shape[1]
    heads_here = q_cols // HEAD_DIM
    store_rows = down_store.shape[0]
    assert req_dev == 1 and store_rows == 1 and ACTIVE % ny == 0

    own_slot = lookup_slots(adapter_ids, adapter_slot)


    down_rows = down_store[0].T.reshape(-1, 128)
    query_rows = query_up_store[0].reshape(-1, 128)
    pair_rows = key_value_store[0].reshape(-1, 128)
    n_down, n_query = down_rows.shape[0], query_rows.shape[0]
    n_row = n_down + n_query + pair_rows.shape[0]
    row = jnp.concatenate([down_rows, query_rows, pair_rows], axis=0)

    plane = gather_over(row, "ry", ny)
    own_slot, plane = lax.optimization_barrier((own_slot, plane))
    slots_all = gather_over(own_slot, ("zh", "zl", "ry"), n_req).reshape(n_req)
    blocks = jnp.stack([states] + [shifted(states, s, n_tp) for s in range(1, n_tp)])
    source = (tp_index - jnp.arange(n_tp, dtype=jnp.int32)) % n_tp
    piece = jnp.take(blocks, source, axis=0)
    plane_req = iz * ny + jnp.arange(ny, dtype=jnp.int32)

    slot_range = jnp.arange(n_req * store_rows, dtype=jnp.int32)
    used = jnp.any(slots_all[:, None] == slot_range[None, :], axis=0).astype(jnp.int32)
    prefix = jnp.sum(
        jnp.where(slot_range[None, :] < slot_range[:, None], used[None, :], 0), axis=1
    )

    per_column = ACTIVE // ny
    plane_slots = plane_req
    wanted = iy + ny * jnp.arange(per_column, dtype=jnp.int32)
    choose = (used[plane_slots][None, :] > 0) & (prefix[plane_slots][None, :] == wanted[:, None])
    column = jnp.sum(
        jnp.where(choose[:, :, None, None], plane[None], jnp.zeros((), plane.dtype)),
        axis=1,
    )
    for axis in ("zh", "zl"):
        copies = gather_over(column, axis, lax.axis_size(axis))
        column = jnp.sum(copies, axis=0)
    dest_k = prefix[slots_all[plane_req]]
    held = column[0]
    for m in range(1, per_column):
        held = jnp.where((dest_k // ny == m)[:, None, None], column[m], held)
    send = jnp.where((dest_k % ny == iy)[:, None, None], held, jnp.zeros((), held.dtype))
    received = lax.all_to_all(send, "ry", 0, 0, tiled=True)
    own_k = prefix[own_slot[0]]
    picked = received[own_k % ny]
    down_t = picked[:n_down].reshape(down_store.shape[2], down_store.shape[1])
    adapter_query = picked[n_down:n_down + n_query].reshape(query_up_store.shape[1:])
    adapter_pair = picked[n_down + n_query:].reshape(key_value_store.shape[1:])

    piece = jnp.transpose(piece, (1, 0, 2)).reshape(rows_total, -1)

    key_value_sum = jnp.dot(piece, key_value_weight, preferred_element_type=jnp.float32)
    from_left = shifted(key_value_sum, 1, n_tp, [(0, 1), (1, 2)])
    from_right = shifted(key_value_sum, -1, n_tp, [(2, 1), (3, 2)])
    from_far = shifted(key_value_sum, 2, n_tp, [(1, 3), (2, 0)])
    key_sum = jnp.where(
        tp_index == 0, key_value_sum, jnp.where(tp_index == 3, from_far, from_left)
    )
    value_sum = jnp.where(
        tp_index == 3, key_value_sum, jnp.where(tp_index == 0, from_far, from_right)
    )

    rank_part = jnp.einsum("kd,sd->ks", down_t, states, preferred_element_type=jnp.float32)
    n_rank, width = rank_part.shape
    lanes = key_value_sum.shape[1]
    rank_rows = rank_part.reshape(-1, lanes)
    n_mid, n_up = rank_rows.shape[0], adapter_pair.shape[0]
    bundle = jnp.concatenate(
        [rank_rows, adapter_pair.astype(jnp.float32)], axis=0
    )
    arrived = gather_over(bundle, "tp", n_tp)
    rank_sum = arrived[0, :n_mid]
    for d in range(1, n_tp):
        rank_sum = rank_sum + arrived[d, :n_mid]
    rank_mid = rank_sum.reshape(n_rank, width).astype(jnp.bfloat16)
    rank_cols = rank_mid.shape[0] // 2
    up_all = arrived[:, n_mid:n_mid + n_up].astype(jnp.bfloat16)
    kv_heads = (n_tp * kv_cols) // 2 // HEAD_DIM
    group_index = tp_index * heads_here // (HEADS // kv_heads)
    key_up = up_all[group_index]
    value_up = up_all[kv_heads + group_index]

    query_total = jnp.dot(piece, query_weight, preferred_element_type=jnp.float32)
    query_addition = jnp.einsum(
        "ks,kc->sc", rank_mid[:rank_cols], adapter_query, preferred_element_type=jnp.float32
    )
    query_plain = query_total + adapter_scale * query_addition
    key_extra = jnp.einsum(
        "ks,kc->sc", rank_mid[rank_cols:], key_up, preferred_element_type=jnp.float32
    )
    value_extra = jnp.einsum(
        "ks,kc->sc", rank_mid[rank_cols:], value_up, preferred_element_type=jnp.float32
    )
    key_block = lax.reduce_precision(
        key_sum + adapter_scale * key_extra, exponent_bits=8, mantissa_bits=7
    )
    value_block = (value_sum + adapter_scale * value_extra).astype(jnp.bfloat16)

    queries = rotate(query_plain.reshape(req_dev, slot_len, heads_here, HEAD_DIM)).astype(
        jnp.bfloat16
    )
    keys_one = rotate(key_block.reshape(req_dev, slot_len, 1, HEAD_DIM)).astype(
        jnp.bfloat16
    )[:, :, 0, :]
    values_one = value_block.reshape(req_dev, slot_len, HEAD_DIM)
    scale = 1.0 / math.sqrt(HEAD_DIM)
    scores = (
        jnp.einsum("rqhd,rkd->rhqk", queries, keys_one, preferred_element_type=jnp.float32) * scale
    )
    position = jnp.arange(slot_len, dtype=jnp.int32)
    allowed = (position[None, None, :] <= position[None, :, None]) & (
        position[None, None, :] < lengths[:, None, None]
    )
    scores = jnp.where(allowed[:, None, :, :], scores, -jnp.inf)
    highest = jnp.max(scores, axis=-1, keepdims=True)
    expo = jnp.exp(scores - highest)
    weights = (expo / jnp.sum(expo, axis=-1, keepdims=True)).astype(jnp.bfloat16)
    context = jnp.einsum("rhqk,rkd->rqhd", weights, values_one, preferred_element_type=jnp.float32)
    live_rows = position[None, :] < lengths[:, None]
    context = jnp.where(live_rows[:, :, None, None], context, 0.0)
    return context.reshape(rows_total, q_cols).astype(jnp.bfloat16)


def solution(mesh):
    n_req = mesh.shape["req"]
    ny = 8 if n_req % 8 == 0 else 1
    n_low = 4 if (n_req // ny) % 4 == 0 else 1
    split = jax.sharding.Mesh(
        mesh.devices.reshape(n_req // ny // n_low, n_low, ny, mesh.shape["tp"]),
        ("zh", "zl", "ry", "tp"),
    )
    req = ("zh", "zl", "ry")
    return jax.shard_map(
        local,
        mesh=split,
        in_specs=(
            P(req, "tp"),
            P(None, "tp"),
            P(None, "tp"),
            P(req),
            P(req),
            P(),
            P(req, "tp", None),
            P(req, None, "tp"),
            P(req, None, "tp"),
        ),
        out_specs=P(req, "tp"),
        check_vma=False,
    )
```

```python
import math

import jax
import jax.numpy as jnp
from jax import lax
from jax.sharding import PartitionSpec as P

HEADS = 12
HEAD_DIM = 128
ACTIVE = 16


adapter_scale = 0.5
rope_base = 100000000000.0


def rotate(field):
    half = field.shape[-1] // 2
    count = field.shape[-3]
    position = jnp.arange(count).astype(jnp.float32)
    inverse = rope_base ** (-(jnp.arange(half).astype(jnp.float32) * 2.0) / field.shape[-1])
    angle = position[:, None] * inverse[None, :]
    cosine = jnp.cos(angle)[:, None, :]
    sine = jnp.sin(angle)[:, None, :]
    first_half = field[..., :half]
    second_half = field[..., half:]
    return jnp.concatenate(
        [first_half * cosine - second_half * sine, second_half * cosine + first_half * sine],
        axis=-1,
    )


def lookup_slots(wanted, adapter_slot):
    table = jnp.arange(adapter_slot.shape[0], dtype=jnp.int32)
    matches = wanted[:, None] == table[None, :]
    return jnp.sum(jnp.where(matches, adapter_slot[None, :], 0), axis=1)


def shifted(x, shift, n, pairs=None, axis="tp"):
    if pairs is None:
        pairs = [(i, (i + shift) % n) for i in range(n)]
    return lax.ppermute(x, axis, pairs)


def gather_over(x, axis, n):
    copies = jnp.broadcast_to(x[None], (n,) + x.shape)
    return lax.all_to_all(copies, axis, 0, 0, tiled=True)


def spread_sum(x, axis, n, radix=4):
    step = 1
    while step < n:
        width = min(radix, n // step)
        assert n % (step * width) == 0
        terms = [x] + [shifted(x, step * m, n, axis=axis) for m in range(1, width)]
        x = sum(terms[1:], terms[0])
        step *= width
    return x


def local(
    states,
    query_weight,
    key_value_weight,
    lengths,
    adapter_ids,
    adapter_slot,
    down_store,
    query_up_store,
    key_value_store,
):
    tp_index = lax.axis_index("tp")
    n_low = lax.axis_size("zl")
    iz = lax.axis_index("zh") * n_low + lax.axis_index("zl")
    iy = lax.axis_index("ry")
    n_tp = lax.axis_size("tp")
    nz = lax.axis_size("zh") * n_low
    ny = lax.axis_size("ry")
    n_req = nz * ny
    me = iz * ny + iy
    req_dev = lengths.shape[0]
    rows_total = states.shape[0]
    slot_len = rows_total // req_dev
    q_cols = query_weight.shape[1]
    kv_cols = key_value_weight.shape[1]
    heads_here = q_cols // HEAD_DIM
    store_rows = down_store.shape[0]
    assert req_dev == 1 and store_rows == 1 and ACTIVE % ny == 0

    own_slot = lookup_slots(adapter_ids, adapter_slot)

    slots_all = gather_over(own_slot, ("zh", "zl", "ry"), n_req).reshape(n_req)

    down_rows = down_store[0].T.reshape(-1, 128)
    query_rows = query_up_store[0].reshape(-1, 128)
    pair_rows = key_value_store[0].reshape(-1, 128)
    n_down, n_query = down_rows.shape[0], query_rows.shape[0]
    n_row = n_down + n_query + pair_rows.shape[0]
    row = jnp.concatenate([down_rows, query_rows, pair_rows], axis=0)

    plane = gather_over(row, "ry", ny)
    blocks = jnp.stack([states] + [shifted(states, s, n_tp) for s in range(1, n_tp)])
    source = (tp_index - jnp.arange(n_tp, dtype=jnp.int32)) % n_tp
    piece = jnp.take(blocks, source, axis=0)
    plane_req = iz * ny + jnp.arange(ny, dtype=jnp.int32)

    slot_range = jnp.arange(n_req * store_rows, dtype=jnp.int32)
    used = jnp.any(slots_all[:, None] == slot_range[None, :], axis=0).astype(jnp.int32)
    prefix = jnp.sum(
        jnp.where(slot_range[None, :] < slot_range[:, None], used[None, :], 0), axis=1
    )

    per_column = ACTIVE // ny
    plane_slots = plane_req
    wanted = iy + ny * jnp.arange(per_column, dtype=jnp.int32)
    choose = (used[plane_slots][None, :] > 0) & (prefix[plane_slots][None, :] == wanted[:, None])
    column = jnp.sum(
        jnp.where(choose[:, :, None, None], plane[None], jnp.zeros((), plane.dtype)),
        axis=1,
    )
    for axis in ("zh", "zl"):
        copies = gather_over(column, axis, lax.axis_size(axis))
        column = jnp.sum(copies, axis=0)
    dest_k = prefix[slots_all[plane_req]]
    held = column[0]
    for m in range(1, per_column):
        held = jnp.where((dest_k // ny == m)[:, None, None], column[m], held)
    send = jnp.where((dest_k % ny == iy)[:, None, None], held, jnp.zeros((), held.dtype))
    received = lax.all_to_all(send, "ry", 0, 0, tiled=True)
    own_k = prefix[own_slot[0]]
    picked = received[own_k % ny]
    down_t = picked[:n_down].reshape(down_store.shape[2], down_store.shape[1])
    adapter_query = picked[n_down:n_down + n_query].reshape(query_up_store.shape[1:])
    adapter_pair = picked[n_down + n_query:].reshape(key_value_store.shape[1:])

    piece = jnp.transpose(piece, (1, 0, 2)).reshape(rows_total, -1)

    key_value_sum = jnp.dot(piece, key_value_weight, preferred_element_type=jnp.float32)
    from_left = shifted(key_value_sum, 1, n_tp, [(0, 1), (1, 2)])
    from_right = shifted(key_value_sum, -1, n_tp, [(2, 1), (3, 2)])
    from_far = shifted(key_value_sum, 2, n_tp, [(1, 3), (2, 0)])
    key_sum = jnp.where(
        tp_index == 0, key_value_sum, jnp.where(tp_index == 3, from_far, from_left)
    )
    value_sum = jnp.where(
        tp_index == 3, key_value_sum, jnp.where(tp_index == 0, from_far, from_right)
    )

    rank_part = jnp.einsum("kd,sd->ks", down_t, states, preferred_element_type=jnp.float32)
    n_rank, width = rank_part.shape
    lanes = key_value_sum.shape[1]
    rank_rows = rank_part.reshape(-1, lanes)
    n_mid, n_up = rank_rows.shape[0], adapter_pair.shape[0]
    bundle = jnp.concatenate(
        [rank_rows, adapter_pair.astype(jnp.float32)], axis=0
    )
    arrived = gather_over(bundle, "tp", n_tp)
    rank_sum = arrived[0, :n_mid]
    for d in range(1, n_tp):
        rank_sum = rank_sum + arrived[d, :n_mid]
    rank_mid = rank_sum.reshape(n_rank, width).astype(jnp.bfloat16)
    rank_cols = rank_mid.shape[0] // 2
    up_all = arrived[:, n_mid:n_mid + n_up].astype(jnp.bfloat16)
    kv_heads = (n_tp * kv_cols) // 2 // HEAD_DIM
    group_index = tp_index * heads_here // (HEADS // kv_heads)
    key_up = up_all[group_index]
    value_up = up_all[kv_heads + group_index]

    query_total = jnp.dot(piece, query_weight, preferred_element_type=jnp.float32)
    query_addition = jnp.einsum(
        "ks,kc->sc", rank_mid[:rank_cols], adapter_query, preferred_element_type=jnp.float32
    )
    query_plain = query_total + adapter_scale * query_addition
    key_extra = jnp.einsum(
        "ks,kc->sc", rank_mid[rank_cols:], key_up, preferred_element_type=jnp.float32
    )
    value_extra = jnp.einsum(
        "ks,kc->sc", rank_mid[rank_cols:], value_up, preferred_element_type=jnp.float32
    )
    key_block = lax.reduce_precision(
        key_sum + adapter_scale * key_extra, exponent_bits=8, mantissa_bits=7
    )
    value_block = (value_sum + adapter_scale * value_extra).astype(jnp.bfloat16)

    queries = rotate(query_plain.reshape(req_dev, slot_len, heads_here, HEAD_DIM)).astype(
        jnp.bfloat16
    )
    keys_one = rotate(key_block.reshape(req_dev, slot_len, 1, HEAD_DIM)).astype(
        jnp.bfloat16
    )[:, :, 0, :]
    values_one = value_block.reshape(req_dev, slot_len, HEAD_DIM)
    scale = 1.0 / math.sqrt(HEAD_DIM)
    scores = (
        jnp.einsum("rqhd,rkd->rhqk", queries, keys_one, preferred_element_type=jnp.float32) * scale
    )
    position = jnp.arange(slot_len, dtype=jnp.int32)
    allowed = (position[None, None, :] <= position[None, :, None]) & (
        position[None, None, :] < lengths[:, None, None]
    )
    scores = jnp.where(allowed[:, None, :, :], scores, -jnp.inf)
    highest = jnp.max(scores, axis=-1, keepdims=True)
    expo = jnp.exp(scores - highest)
    weights = (expo / jnp.sum(expo, axis=-1, keepdims=True)).astype(jnp.bfloat16)
    context = jnp.einsum("rhqk,rkd->rqhd", weights, values_one, preferred_element_type=jnp.float32)
    live_rows = position[None, :] < lengths[:, None]
    context = jnp.where(live_rows[:, :, None, None], context, 0.0)
    return context.reshape(rows_total, q_cols).astype(jnp.bfloat16)


def solution(mesh):
    n_req = mesh.shape["req"]
    ny = 8 if n_req % 8 == 0 else 1
    n_low = 2 if (n_req // ny) % 2 == 0 else 1
    split = jax.sharding.Mesh(
        mesh.devices.reshape(n_req // ny // n_low, n_low, ny, mesh.shape["tp"]),
        ("zh", "zl", "ry", "tp"),
    )
    req = ("zh", "zl", "ry")
    return jax.shard_map(
        local,
        mesh=split,
        in_specs=(
            P(req, "tp"),
            P(None, "tp"),
            P(None, "tp"),
            P(req),
            P(req),
            P(),
            P(req, "tp", None),
            P(req, None, "tp"),
            P(req, None, "tp"),
        ),
        out_specs=P(req, "tp"),
        check_vma=False,
    )
```

```python
import math

import jax
import jax.numpy as jnp
from jax import lax
from jax.sharding import PartitionSpec as P

HEADS = 12
HEAD_DIM = 128
ACTIVE = 16


adapter_scale = 0.5
rope_base = 100000000000.0


def rotate(field):
    half = field.shape[-1] // 2
    count = field.shape[-3]
    position = jnp.arange(count).astype(jnp.float32)
    inverse = rope_base ** (-(jnp.arange(half).astype(jnp.float32) * 2.0) / field.shape[-1])
    angle = position[:, None] * inverse[None, :]
    cosine = jnp.cos(angle)[:, None, :]
    sine = jnp.sin(angle)[:, None, :]
    first_half = field[..., :half]
    second_half = field[..., half:]
    return jnp.concatenate(
        [first_half * cosine - second_half * sine, second_half * cosine + first_half * sine],
        axis=-1,
    )


def lookup_slots(wanted, adapter_slot):
    table = jnp.arange(adapter_slot.shape[0], dtype=jnp.int32)
    matches = wanted[:, None] == table[None, :]
    return jnp.sum(jnp.where(matches, adapter_slot[None, :], 0), axis=1)


def shifted(x, shift, n, pairs=None, axis="tp"):
    if pairs is None:
        pairs = [(i, (i + shift) % n) for i in range(n)]
    return lax.ppermute(x, axis, pairs)


def gather_over(x, axis, n):
    copies = jnp.broadcast_to(x[None], (n,) + x.shape)
    return lax.all_to_all(copies, axis, 0, 0, tiled=True)


def spread_sum(x, axis, n, radix=4):
    step = 1
    while step < n:
        width = min(radix, n // step)
        assert n % (step * width) == 0
        terms = [x] + [shifted(x, step * m, n, axis=axis) for m in range(1, width)]
        x = sum(terms[1:], terms[0])
        step *= width
    return x


def local(
    states,
    query_weight,
    key_value_weight,
    lengths,
    adapter_ids,
    adapter_slot,
    down_store,
    query_up_store,
    key_value_store,
):
    tp_index = lax.axis_index("tp")
    n_low = lax.axis_size("zl")
    iz = lax.axis_index("zh") * n_low + lax.axis_index("zl")
    iy = lax.axis_index("ry")
    n_tp = lax.axis_size("tp")
    nz = lax.axis_size("zh") * n_low
    ny = lax.axis_size("ry")
    n_req = nz * ny
    me = iz * ny + iy
    req_dev = lengths.shape[0]
    rows_total = states.shape[0]
    slot_len = rows_total // req_dev
    q_cols = query_weight.shape[1]
    kv_cols = key_value_weight.shape[1]
    heads_here = q_cols // HEAD_DIM
    store_rows = down_store.shape[0]
    assert req_dev == 1 and store_rows == 1 and ACTIVE % ny == 0

    own_slot = lookup_slots(adapter_ids, adapter_slot)

    slots_all = gather_over(own_slot, ("zh", "zl", "ry"), n_req).reshape(n_req)

    down_rows = down_store[0].T.reshape(-1, 128)
    query_rows = query_up_store[0].reshape(-1, 128)
    pair_rows = key_value_store[0].reshape(-1, 128)
    n_down, n_query = down_rows.shape[0], query_rows.shape[0]
    n_row = n_down + n_query + pair_rows.shape[0]
    row = jnp.concatenate([down_rows, query_rows, pair_rows], axis=0)

    plane = gather_over(row, "ry", ny)
    blocks = jnp.stack([states] + [shifted(states, s, n_tp) for s in range(1, n_tp)])
    source = (tp_index - jnp.arange(n_tp, dtype=jnp.int32)) % n_tp
    piece = jnp.take(blocks, source, axis=0)
    plane_req = iz * ny + jnp.arange(ny, dtype=jnp.int32)

    slot_range = jnp.arange(n_req * store_rows, dtype=jnp.int32)
    used = jnp.any(slots_all[:, None] == slot_range[None, :], axis=0).astype(jnp.int32)
    prefix = jnp.sum(
        jnp.where(slot_range[None, :] < slot_range[:, None], used[None, :], 0), axis=1
    )

    per_column = ACTIVE // ny
    plane_slots = plane_req
    wanted = iy + ny * jnp.arange(per_column, dtype=jnp.int32)
    choose = (used[plane_slots][None, :] > 0) & (prefix[plane_slots][None, :] == wanted[:, None])
    column = jnp.sum(
        jnp.where(choose[:, :, None, None], plane[None], jnp.zeros((), plane.dtype)),
        axis=1,
    )
    copies = gather_over(column, "zh", nz // n_low)
    column = jnp.sum(copies, axis=0)
    group = n_low * ny
    dest_req = lax.axis_index("zh") * group + jnp.arange(group, dtype=jnp.int32)
    dest_k = prefix[slots_all[dest_req]]
    held = column[0]
    for m in range(1, per_column):
        held = jnp.where((dest_k // ny == m)[:, None, None], column[m], held)
    send = jnp.where((dest_k % ny == iy)[:, None, None], held, jnp.zeros((), held.dtype))
    received = lax.all_to_all(send, ("zl", "ry"), 0, 0, tiled=True)
    own_k = prefix[own_slot[0]]
    picked = jnp.sum(received, axis=0)
    down_t = picked[:n_down].reshape(down_store.shape[2], down_store.shape[1])
    adapter_query = picked[n_down:n_down + n_query].reshape(query_up_store.shape[1:])
    adapter_pair = picked[n_down + n_query:].reshape(key_value_store.shape[1:])

    piece = jnp.transpose(piece, (1, 0, 2)).reshape(rows_total, -1)

    key_value_sum = jnp.dot(piece, key_value_weight, preferred_element_type=jnp.float32)
    from_left = shifted(key_value_sum, 1, n_tp, [(0, 1), (1, 2)])
    from_right = shifted(key_value_sum, -1, n_tp, [(2, 1), (3, 2)])
    from_far = shifted(key_value_sum, 2, n_tp, [(1, 3), (2, 0)])
    key_sum = jnp.where(
        tp_index == 0, key_value_sum, jnp.where(tp_index == 3, from_far, from_left)
    )
    value_sum = jnp.where(
        tp_index == 3, key_value_sum, jnp.where(tp_index == 0, from_far, from_right)
    )

    rank_part = jnp.einsum("kd,sd->ks", down_t, states, preferred_element_type=jnp.float32)
    n_rank, width = rank_part.shape
    lanes = key_value_sum.shape[1]
    rank_rows = rank_part.reshape(-1, lanes)
    n_mid, n_up = rank_rows.shape[0], adapter_pair.shape[0]
    bundle = jnp.concatenate(
        [rank_rows, adapter_pair.astype(jnp.float32)], axis=0
    )
    arrived = gather_over(bundle, "tp", n_tp)
    rank_sum = arrived[0, :n_mid]
    for d in range(1, n_tp):
        rank_sum = rank_sum + arrived[d, :n_mid]
    rank_mid = rank_sum.reshape(n_rank, width).astype(jnp.bfloat16)
    rank_cols = rank_mid.shape[0] // 2
    up_all = arrived[:, n_mid:n_mid + n_up].astype(jnp.bfloat16)
    kv_heads = (n_tp * kv_cols) // 2 // HEAD_DIM
    group_index = tp_index * heads_here // (HEADS // kv_heads)
    key_up = up_all[group_index]
    value_up = up_all[kv_heads + group_index]

    query_total = jnp.dot(piece, query_weight, preferred_element_type=jnp.float32)
    query_addition = jnp.einsum(
        "ks,kc->sc", rank_mid[:rank_cols], adapter_query, preferred_element_type=jnp.float32
    )
    query_plain = query_total + adapter_scale * query_addition
    key_extra = jnp.einsum(
        "ks,kc->sc", rank_mid[rank_cols:], key_up, preferred_element_type=jnp.float32
    )
    value_extra = jnp.einsum(
        "ks,kc->sc", rank_mid[rank_cols:], value_up, preferred_element_type=jnp.float32
    )
    key_block = lax.reduce_precision(
        key_sum + adapter_scale * key_extra, exponent_bits=8, mantissa_bits=7
    )
    value_block = (value_sum + adapter_scale * value_extra).astype(jnp.bfloat16)

    queries = rotate(query_plain.reshape(req_dev, slot_len, heads_here, HEAD_DIM)).astype(
        jnp.bfloat16
    )
    keys_one = rotate(key_block.reshape(req_dev, slot_len, 1, HEAD_DIM)).astype(
        jnp.bfloat16
    )[:, :, 0, :]
    values_one = value_block.reshape(req_dev, slot_len, HEAD_DIM)
    scale = 1.0 / math.sqrt(HEAD_DIM)
    scores = (
        jnp.einsum("rqhd,rkd->rhqk", queries, keys_one, preferred_element_type=jnp.float32) * scale
    )
    position = jnp.arange(slot_len, dtype=jnp.int32)
    allowed = (position[None, None, :] <= position[None, :, None]) & (
        position[None, None, :] < lengths[:, None, None]
    )
    scores = jnp.where(allowed[:, None, :, :], scores, -jnp.inf)
    highest = jnp.max(scores, axis=-1, keepdims=True)
    expo = jnp.exp(scores - highest)
    weights = (expo / jnp.sum(expo, axis=-1, keepdims=True)).astype(jnp.bfloat16)
    context = jnp.einsum("rhqk,rkd->rqhd", weights, values_one, preferred_element_type=jnp.float32)
    live_rows = position[None, :] < lengths[:, None]
    context = jnp.where(live_rows[:, :, None, None], context, 0.0)
    return context.reshape(rows_total, q_cols).astype(jnp.bfloat16)


def solution(mesh):
    n_req = mesh.shape["req"]
    ny = 8 if n_req % 8 == 0 else 1
    n_low = 4 if (n_req // ny) % 4 == 0 else 1
    split = jax.sharding.Mesh(
        mesh.devices.reshape(n_req // ny // n_low, n_low, ny, mesh.shape["tp"]),
        ("zh", "zl", "ry", "tp"),
    )
    req = ("zh", "zl", "ry")
    return jax.shard_map(
        local,
        mesh=split,
        in_specs=(
            P(req, "tp"),
            P(None, "tp"),
            P(None, "tp"),
            P(req),
            P(req),
            P(),
            P(req, "tp", None),
            P(req, None, "tp"),
            P(req, None, "tp"),
        ),
        out_specs=P(req, "tp"),
        check_vma=False,
    )
```
